128 devices in a mesh: sec: 4 (over z_hi, core), pts: 32 (over x, z_lo, y).
Axes of the slice: x: 4, y: 4, z: 4 (z_hi: 2, z_lo: 2; z = z_hi * 2 + z_lo), core: 2. Of those that a mesh axis runs over, the one named last changes fastest.
Arguments:
- points: bfloat16 [4, 32768, 1024], P('sec', 'pts'), may hold values from -10 to 10
- counts: int32 [4, 32], P('sec', 'pts'), may hold values from 256 to 1024, as said below
- input_gain: float32 [4, 1024], P('sec'), may hold values from 0.1 to 1.9
- key_weight: bfloat16 [4, 1024, 1024], P('sec', 'pts'), may hold values from -0.375 to 0.375
- value_weight: bfloat16 [4, 1024, 1024], P('sec', 'pts'), may hold values from -0.375 to 0.375
- query_weight: bfloat16 [1024, 1024], replicated, may hold values from -0.1875 to 0.1875
- output_weight: bfloat16 [1024, 1024], replicated, may hold values from -0.75 to 0.75
- middle_gain: float32 [1024], replicated, may hold values from 0.1 to 1.9
- up_weight: bfloat16 [1024, 4096], P(None, 'sec'), may hold values from -0.1875 to 0.1875
- down_weight: bfloat16 [4096, 1024], P('sec'), may hold values from -0.09375 to 0.09375
Outputs:
- updated: bfloat16 [32768, 1024], P('pts', 'sec')
The draws below stay inside these ranges and needn't reach their ends.
Inputs may be any that keep to these rules, and one draw needn't show every extreme that they name: `counts`: each block has 1024 slots; in every section some block is full.
All inputs are finite; a program needn't handle non-finite values.
Results may differ from the reference program's by a relative error of at most 0.0049.
Values may be sent and summed in bfloat16 or wider, within the bound.
No kernel may reach another device: no remote copies, remote signals or barrier semaphores. Data moves between devices by JAX's collectives and lax.ppermute only.
A program may use at most 128 MiB of HBM per device.

```python
import jax
import jax.numpy as jnp
from jax import lax

HEADS = 8
HEAD_DIM = 128
D = 1024
FF = 4096
ROWS = 1024
PTS = 32768
N_SEC = 4


def draw_points(key, part):
    base_key, shift_key = jax.random.split(jax.random.fold_in(key, 11))
    region = ROWS // 4
    regions = PTS // region
    base = jnp.clip(jax.random.normal(base_key, (4, PTS, D), jnp.float32), -4.0, 4.0)
    spread = 1.5
    offsets = jnp.clip(jax.random.normal(shift_key, (4, regions, D), jnp.float32), -3.0, 3.0) * spread
    return (base + jnp.repeat(offsets, region, axis=1)).astype(jnp.bfloat16)


def draw_counts(key, part):
    fill_key, spot_key = jax.random.split(jax.random.fold_in(key, 23))
    blocks = PTS // ROWS
    values = jax.random.randint(fill_key, (4, blocks), ROWS // 4, ROWS + 1)
    spots = jax.random.randint(spot_key, (4, 1), 0, blocks)
    full = jnp.arange(blocks)[None, :] == spots
    return jnp.where(full, ROWS, values).astype(jnp.int32)


def strengthened(entries, rng, source, target, parts, factor):
    owner, partner = [(jnp.arange(entries.shape[dim]) // (entries.shape[dim] // parts)).reshape([-1 if axis == dim else 1 for axis in range(entries.ndim)]) for dim in (source, target)]
    chosen = jax.random.permutation(rng, parts)[partner]
    strong = (owner == chosen) | (owner == (partner + parts // 2) % parts)
    return jnp.where(strong, factor * entries, entries)


def level_of(own_key, shape, shards, smallest, largest):
    factor_of = 1.0
    for axis_at, parts in shards:
        draws = jax.random.uniform(jax.random.fold_in(jax.random.fold_in(own_key, 6), axis_at), (parts,), jnp.float32, smallest / len(shards), largest / len(shards))
        factor_of = factor_of * jnp.repeat(jnp.exp(draws), shape[axis_at] // parts).reshape((-1,) + (1,) * (len(shape) - 1 - axis_at))
    return factor_of


def scatter_about(own_key, extent, scale, bound, cuts=(), held_as=jnp.bfloat16):
    entries = scale * jax.random.normal(own_key, extent, jnp.float32)
    if cuts:
        entries = entries * level_of(own_key, extent, cuts, -0.22, 0.18)
    return jnp.clip(entries, -bound, bound).astype(held_as)


def gaussian_with(stream_key, extent, scale, most, cuts, heavy, held_as=jnp.bfloat16):
    result = scale * jax.random.normal(stream_key, extent, jnp.float32)
    if cuts:
        result = result * level_of(stream_key, extent, cuts, -0.22, 0.18)
    return jnp.clip(strengthened(result, jax.random.fold_in(stream_key, 3), *heavy), -most, most).astype(held_as)


def setup_inputs(seed: int = 0) -> dict:
    arg_keys = jax.random.split(jax.random.key(seed), 11)
    return {
        "points": draw_points(jax.random.fold_in(arg_keys[10], 71), 0),
        "counts": draw_counts(jax.random.fold_in(arg_keys[10], 71), 0),
        "input_gain": jnp.clip(1.0 + 0.18 * jax.random.normal(arg_keys[2], (N_SEC, D), jnp.float32), 0.1, 1.9),
        "key_weight": gaussian_with(arg_keys[3], (N_SEC, D, D), D ** -0.5, 0.375, ((0, 4), (1, 32)), (1, 2, 32, 2.75)),
        "value_weight": gaussian_with(arg_keys[4], (N_SEC, D, D), D ** -0.5, 0.375, ((0, 4), (1, 32)), (1, 2, 32, 2.75)),
        "query_weight": scatter_about(arg_keys[5], (D, D), D ** -0.5, 0.1875),
        "output_weight": scatter_about(arg_keys[6], (D, D), (D // 16) ** -0.5, 0.75),
        "middle_gain": jnp.clip(1.0 + 0.18 * jax.random.normal(arg_keys[7], (D,), jnp.float32), 0.1, 1.9),
        "up_weight": scatter_about(arg_keys[8], (D, FF), D ** -0.5, 0.1875, ((1, 4),)),
        "down_weight": scatter_about(arg_keys[9], (FF, D), FF ** -0.5, 0.09375, ((0, 4),)),
    }


def layer_normalizer(values, gain):
    mean = lax.optimization_barrier(jnp.mean(values, axis=-1, keepdims=True))
    centred = values - mean
    spread = lax.optimization_barrier(jnp.mean(centred * centred, axis=-1, keepdims=True))
    return centred * lax.rsqrt(spread + 1e-05) * gain

def feature_map(values):
    return jax.nn.elu(values) + 1.0

def reference(points, counts, input_gain, key_weight, value_weight, query_weight, output_weight, middle_gain, up_weight, down_weight):
    sections = points.shape[0]
    slot_index = (jnp.arange(PTS) % ROWS).astype(jnp.int32)
    valid = slot_index[None, :] < jnp.repeat(counts, ROWS, axis=1)
    query_normed = layer_normalizer(points[sections - 1].astype(jnp.float32), input_gain[sections - 1]).astype(jnp.bfloat16)
    query_feats = feature_map(jnp.dot(query_normed, query_weight, preferred_element_type=jnp.float32)).astype(jnp.bfloat16)
    query_feats = lax.optimization_barrier(query_feats)
    per_head_queries = query_feats.astype(jnp.float32).reshape(PTS, HEADS, HEAD_DIM)
    attended = jnp.zeros((PTS, HEADS, HEAD_DIM), jnp.float32)
    for section in range(sections):
        normed = layer_normalizer(points[section].astype(jnp.float32), input_gain[section]).astype(jnp.bfloat16)
        key_feats = feature_map(jnp.dot(normed, key_weight[section], preferred_element_type=jnp.float32)).astype(jnp.bfloat16)
        key_feats = jnp.where(valid[section][:, None], key_feats, jnp.zeros_like(key_feats))
        value_rows = jnp.dot(normed, value_weight[section], preferred_element_type=jnp.float32).astype(jnp.bfloat16)
        per_head_keys = key_feats.astype(jnp.float32).reshape(PTS, HEADS, HEAD_DIM)
        per_head_values = value_rows.astype(jnp.float32).reshape(PTS, HEADS, HEAD_DIM)
        state_matrices = jnp.einsum('yzl,yzn->zln', per_head_keys, per_head_values)
        totals = lax.optimization_barrier(jnp.sum(per_head_keys, axis=0))
        numerator = jnp.einsum('upz,pzm->upm', per_head_queries, state_matrices, precision=lax.Precision.HIGHEST)
        denom = jnp.einsum('rhk,hk->rh', per_head_queries, totals, precision=lax.Precision.HIGHEST)
        attended = attended + numerator / denom[:, :, None]
    attended = attended.reshape(PTS, HEADS * HEAD_DIM).astype(jnp.bfloat16)
    mixed = points[sections - 1].astype(jnp.float32) + jnp.dot(attended, output_weight, preferred_element_type=jnp.float32)
    centred = layer_normalizer(mixed, middle_gain).astype(jnp.bfloat16)
    hidden = jax.nn.gelu(jnp.dot(centred, up_weight, preferred_element_type=jnp.float32), approximate=True).astype(jnp.bfloat16)
    return (mixed + jnp.dot(hidden, down_weight, preferred_element_type=jnp.float32)).astype(jnp.bfloat16)
```

```python
import jax
import jax.numpy as jnp
from jax import lax
from jax.sharding import PartitionSpec as P

HEAD_DIM = 128


def layer_normalizer(values, gain):
    mean = jnp.mean(values, axis=-1, keepdims=True)
    centred = values - mean
    spread = jnp.mean(centred * centred, axis=-1, keepdims=True)
    return centred * lax.rsqrt(spread + 1e-05) * gain


def feature_map(values):
    return jax.nn.elu(values) + 1.0


def from_last(value, axis, sections):
    me = lax.axis_index(axis)
    last = sections - 1
    if sections != 4:
        out = value
        for target in range(last):
            got = lax.ppermute(value, axis, [(last, target)])
            out = jnp.where(me == target, got, out)
        return out
    far = lax.ppermute(value, axis, [(3, 1)])
    near = lax.ppermute(value, axis, [(3, 2)])
    farther = lax.ppermute(far, axis, [(1, 0)])
    return jnp.where(
        me == 3, value, jnp.where(me == 2, near, jnp.where(me == 1, far, farther))
    )


def gather_a2a(value, axis, count):
    spread = jnp.broadcast_to(value[None], (count,) + value.shape)
    return lax.all_to_all(spread, axis, 0, 0, tiled=False)


def on_device(
    points,
    counts,
    input_gain,
    key_weight,
    value_weight,
    query_weight,
    output_weight,
    middle_gain,
    up_weight,
    down_weight,
):
    block = points[0]
    rows = block.shape[0]
    width = block.shape[1]
    heads = width // HEAD_DIM
    sections = lax.axis_size("sec")
    blocks = lax.axis_size("pts")
    me = lax.axis_index("sec")

    query_block = from_last(block, "sec", sections)
    query_gain = from_last(input_gain[0], "sec", sections)

    stacked = jnp.concatenate([key_weight[0], value_weight[0]], axis=1)
    weights = gather_a2a(stacked, "pts", blocks).reshape(width, 2 * width)

    normed = layer_normalizer(block.astype(jnp.float32), input_gain[0]).astype(jnp.bfloat16)
    projected = jnp.dot(normed, weights, preferred_element_type=jnp.float32)
    valid = jnp.arange(rows) < counts[0, 0]
    key_feats = feature_map(projected[:, :width]).astype(jnp.bfloat16)
    key_feats = jnp.where(valid[:, None], key_feats, jnp.zeros_like(key_feats))
    value_rows = projected[:, width:].astype(jnp.bfloat16)
    local_state = jnp.einsum(
        "yzl,yzn->zln",
        key_feats.reshape(rows, heads, HEAD_DIM),
        value_rows.reshape(rows, heads, HEAD_DIM),
        preferred_element_type=jnp.float32,
    ).reshape(width, HEAD_DIM)
    local_total = jnp.sum(key_feats.astype(jnp.float32), axis=0).reshape(heads, HEAD_DIM)

    packed_rows = width + heads
    piece = -(-packed_rows // blocks)
    packed = jnp.concatenate(
        [
            local_state,
            local_total,
            jnp.zeros((piece * blocks - packed_rows, HEAD_DIM), jnp.float32),
        ],
        axis=0,
    ).reshape(blocks, piece, HEAD_DIM)
    reduced = jnp.sum(lax.all_to_all(packed, "pts", 0, 0, tiled=False), axis=0)
    by_section = gather_a2a(reduced, "sec", sections)
    whole = gather_a2a(by_section, "pts", blocks)
    whole = whole.transpose(1, 0, 2, 3).reshape(sections, blocks * piece, HEAD_DIM)
    state_heads = whole[:, :width].reshape(sections, heads, HEAD_DIM, HEAD_DIM)
    total_heads = whole[:, width:packed_rows].reshape(sections, heads, HEAD_DIM)

    query_normed = layer_normalizer(query_block.astype(jnp.float32), query_gain).astype(
        jnp.bfloat16
    )
    query_feats = feature_map(
        jnp.dot(query_normed, query_weight, preferred_element_type=jnp.float32)
    ).astype(jnp.bfloat16)
    per_head_queries = query_feats.astype(jnp.float32).reshape(rows, heads, HEAD_DIM)
    numerator = jnp.einsum(
        "rhk,shkv->srhv", per_head_queries, state_heads, precision=lax.Precision.HIGHEST
    )
    denom = jnp.einsum(
        "rhk,shk->srh", per_head_queries, total_heads, precision=lax.Precision.HIGHEST
    )
    attended = (
        jnp.sum(numerator / denom[:, :, :, None], axis=0).reshape(rows, width).astype(jnp.bfloat16)
    )
    mixed = query_block.astype(jnp.float32) + jnp.dot(
        attended, output_weight, preferred_element_type=jnp.float32
    )
    centred = layer_normalizer(mixed, middle_gain).astype(jnp.bfloat16)
    hidden = jax.nn.gelu(
        jnp.dot(centred, up_weight, preferred_element_type=jnp.float32), approximate=True
    ).astype(jnp.bfloat16)
    term = jnp.dot(hidden, down_weight, preferred_element_type=jnp.float32)
    share = width // sections
    parts = term.astype(jnp.bfloat16).reshape(rows, sections, share).transpose(1, 0, 2)
    summed = jnp.sum(lax.all_to_all(parts, "sec", 0, 0, tiled=False).astype(jnp.float32), axis=0)
    own_mixed = lax.dynamic_slice_in_dim(mixed, me * share, share, axis=1)
    return (own_mixed + summed).astype(jnp.bfloat16)


def solution(mesh):
    placed = (
        P("sec", "pts", None),
        P("sec", "pts"),
        P("sec", None),
        P("sec", "pts", None),
        P("sec", "pts", None),
        P(),
        P(),
        P(),
        P(None, "sec"),
        P("sec", None),
    )
    return jax.shard_map(
        on_device, mesh=mesh, in_specs=placed, out_specs=P("pts", "sec"), check_vma=False
    )
```

```python
import jax
import jax.numpy as jnp
from jax import lax
from jax.sharding import PartitionSpec as P

HEAD_DIM = 128


def layer_normalizer(values, gain):
    mean = jnp.mean(values, axis=-1, keepdims=True)
    centred = values - mean
    spread = jnp.mean(centred * centred, axis=-1, keepdims=True)
    return centred * lax.rsqrt(spread + 1e-05) * gain


def feature_map(values):
    return jax.nn.elu(values) + 1.0


def from_last(value, axis, sections):
    me = lax.axis_index(axis)
    last = sections - 1
    if sections != 4:
        out = value
        for target in range(last):
            got = lax.ppermute(value, axis, [(last, target)])
            out = jnp.where(me == target, got, out)
        return out
    far = lax.ppermute(value, axis, [(3, 1)])
    near = lax.ppermute(value, axis, [(3, 2)])
    farther = lax.ppermute(far, axis, [(1, 0)])
    return jnp.where(
        me == 3, value, jnp.where(me == 2, near, jnp.where(me == 1, far, farther))
    )


def gather_a2a(value, axis, count):
    spread = jnp.broadcast_to(value[None], (count,) + value.shape)
    return lax.all_to_all(spread, axis, 0, 0, tiled=False)


def on_device(
    points,
    counts,
    input_gain,
    key_weight,
    value_weight,
    query_weight,
    output_weight,
    middle_gain,
    up_weight,
    down_weight,
):
    block = points[0]
    rows = block.shape[0]
    width = block.shape[1]
    heads = width // HEAD_DIM
    sections = lax.axis_size("sec")
    blocks = lax.axis_size("pts")
    me = lax.axis_index("sec")

    query_block = from_last(block, "sec", sections)
    query_gain = from_last(input_gain[0], "sec", sections)

    stacked = jnp.concatenate([key_weight[0], value_weight[0]], axis=1)
    weights = gather_a2a(stacked, "pts", blocks).reshape(width, 2 * width)

    normed = layer_normalizer(block.astype(jnp.float32), input_gain[0]).astype(jnp.bfloat16)
    projected = jnp.dot(normed, weights, preferred_element_type=jnp.float32)
    valid = jnp.arange(rows) < counts[0, 0]
    key_feats = feature_map(projected[:, :width]).astype(jnp.bfloat16)
    key_feats = jnp.where(valid[:, None], key_feats, jnp.zeros_like(key_feats))
    value_rows = projected[:, width:].astype(jnp.bfloat16)
    local_state = jnp.einsum(
        "yzl,yzn->zln",
        key_feats.reshape(rows, heads, HEAD_DIM),
        value_rows.reshape(rows, heads, HEAD_DIM),
        preferred_element_type=jnp.float32,
    ).reshape(width, HEAD_DIM)
    local_total = jnp.sum(key_feats.astype(jnp.float32), axis=0).reshape(heads, HEAD_DIM)

    packed_rows = width + heads
    piece = -(-packed_rows // blocks)
    packed = jnp.concatenate(
        [
            local_state,
            local_total,
            jnp.zeros((piece * blocks - packed_rows, HEAD_DIM), jnp.float32),
        ],
        axis=0,
    ).reshape(blocks, piece, HEAD_DIM)
    reduced = jnp.sum(lax.all_to_all(packed, "pts", 0, 0, tiled=False), axis=0)
    by_section = gather_a2a(reduced, "sec", sections)
    whole = gather_a2a(by_section, "pts", blocks)
    whole = whole.transpose(1, 0, 2, 3).reshape(sections, blocks * piece, HEAD_DIM)
    state_heads = whole[:, :width].reshape(sections, heads, HEAD_DIM, HEAD_DIM)
    total_heads = whole[:, width:packed_rows].reshape(sections, heads, HEAD_DIM)

    query_normed = layer_normalizer(query_block.astype(jnp.float32), query_gain).astype(
        jnp.bfloat16
    )
    query_feats = feature_map(
        jnp.dot(query_normed, query_weight, preferred_element_type=jnp.float32)
    ).astype(jnp.bfloat16)
    per_head_queries = query_feats.reshape(rows, heads, HEAD_DIM)

    joined = jnp.concatenate(
        [
            state_heads.transpose(1, 2, 0, 3).reshape(heads, HEAD_DIM, sections * HEAD_DIM),
            total_heads.transpose(1, 2, 0),
            jnp.zeros((heads, HEAD_DIM, HEAD_DIM - sections), jnp.float32),
        ],
        axis=2,
    )
    high = joined.astype(jnp.bfloat16)
    rest = joined - high.astype(jnp.float32)
    middle = rest.astype(jnp.bfloat16)
    low = (rest - middle.astype(jnp.float32)).astype(jnp.bfloat16)

    share = width // sections
    chunks = 2 if rows % 16 == 0 else 1
    step = rows // chunks
    outs = []
    for c in range(chunks):
        queries = per_head_queries[c * step : (c + 1) * step]
        products = sum(
            jnp.einsum("rhk,hkc->rhc", queries, term, preferred_element_type=jnp.float32)
            for term in (high, middle, low)
        )
        numerator = products[:, :, : sections * HEAD_DIM].reshape(step, heads, sections, HEAD_DIM)
        denom = products[:, :, sections * HEAD_DIM : sections * HEAD_DIM + sections]
        attended = (
            jnp.sum(numerator / denom[:, :, :, None], axis=2)
            .reshape(step, width)
            .astype(jnp.bfloat16)
        )
        mixed = query_block[c * step : (c + 1) * step].astype(jnp.float32) + jnp.dot(
            attended, output_weight, preferred_element_type=jnp.float32
        )
        centred = layer_normalizer(mixed, middle_gain).astype(jnp.bfloat16)
        hidden = jax.nn.gelu(
            jnp.dot(centred, up_weight, preferred_element_type=jnp.float32), approximate=True
        ).astype(jnp.bfloat16)
        term = jnp.dot(hidden, down_weight, preferred_element_type=jnp.float32)
        parts = term.astype(jnp.bfloat16).reshape(step, sections, share).transpose(1, 0, 2)
        summed = jnp.sum(
            lax.all_to_all(parts, "sec", 0, 0, tiled=False).astype(jnp.float32), axis=0
        )
        own_mixed = lax.dynamic_slice_in_dim(mixed, me * share, share, axis=1)
        outs.append((own_mixed + summed).astype(jnp.bfloat16))
    return jnp.concatenate(outs, axis=0)


def solution(mesh):
    placed = (
        P("sec", "pts", None),
        P("sec", "pts"),
        P("sec", None),
        P("sec", "pts", None),
        P("sec", "pts", None),
        P(),
        P(),
        P(),
        P(None, "sec"),
        P("sec", None),
    )
    return jax.shard_map(
        on_device, mesh=mesh, in_specs=placed, out_specs=P("pts", "sec"), check_vma=False
    )
```

```python
import jax
import jax.numpy as jnp
from jax import lax
from jax.sharding import PartitionSpec as P

HEAD_DIM = 128


def layer_normalizer(values, gain):
    mean = jnp.mean(values, axis=-1, keepdims=True)
    centred = values - mean
    spread = jnp.mean(centred * centred, axis=-1, keepdims=True)
    return centred * lax.rsqrt(spread + 1e-05) * gain


def feature_map(values):
    return jax.nn.elu(values) + 1.0


def from_last(value, axis, sections):
    me = lax.axis_index(axis)
    last = sections - 1
    if sections != 4:
        out = value
        for target in range(last):
            got = lax.ppermute(value, axis, [(last, target)])
            out = jnp.where(me == target, got, out)
        return out
    far = lax.ppermute(value, axis, [(3, 1)])
    near = lax.ppermute(value, axis, [(3, 2)])
    farther = lax.ppermute(far, axis, [(1, 0)])
    return jnp.where(
        me == 3, value, jnp.where(me == 2, near, jnp.where(me == 1, far, farther))
    )


def gather_a2a(value, axis, count):
    spread = jnp.broadcast_to(value[None], (count,) + value.shape)
    return lax.all_to_all(spread, axis, 0, 0, tiled=False)


def on_device(
    points,
    counts,
    input_gain,
    key_weight,
    value_weight,
    query_weight,
    output_weight,
    middle_gain,
    up_weight,
    down_weight,
):
    block = points[0]
    rows = block.shape[0]
    width = block.shape[1]
    heads = width // HEAD_DIM
    sections = lax.axis_size("sec")
    blocks = lax.axis_size("pts")
    me = lax.axis_index("sec")

    query_block = from_last(block, "sec", sections)
    query_gain = from_last(input_gain[0], "sec", sections)

    stacked = jnp.concatenate([key_weight[0], value_weight[0]], axis=1)
    weights = gather_a2a(stacked, "pts", blocks).reshape(width, 2 * width)

    normed = layer_normalizer(block.astype(jnp.float32), input_gain[0]).astype(jnp.bfloat16)
    projected = jnp.dot(normed, weights, preferred_element_type=jnp.float32)
    valid = jnp.arange(rows) < counts[0, 0]
    key_feats = feature_map(projected[:, :width]).astype(jnp.bfloat16)
    key_feats = jnp.where(valid[:, None], key_feats, jnp.zeros_like(key_feats))
    value_rows = projected[:, width:].astype(jnp.bfloat16)
    local_state = jnp.einsum(
        "yzl,yzn->zln",
        key_feats.reshape(rows, heads, HEAD_DIM),
        value_rows.reshape(rows, heads, HEAD_DIM),
        preferred_element_type=jnp.float32,
    ).reshape(width, HEAD_DIM)
    local_total = jnp.sum(key_feats.astype(jnp.float32), axis=0).reshape(heads, HEAD_DIM)

    packed_rows = width + heads
    piece = -(-packed_rows // blocks)
    packed = jnp.concatenate(
        [
            local_state,
            local_total,
            jnp.zeros((piece * blocks - packed_rows, HEAD_DIM), jnp.float32),
        ],
        axis=0,
    ).reshape(blocks, piece, HEAD_DIM)
    reduced = jnp.sum(lax.all_to_all(packed, "pts", 0, 0, tiled=False), axis=0)
    by_section = gather_a2a(reduced, "sec", sections)
    whole = gather_a2a(by_section, "pts", blocks)
    whole = whole.transpose(1, 0, 2, 3).reshape(sections, blocks * piece, HEAD_DIM)
    state_heads = whole[:, :width].reshape(sections, heads, HEAD_DIM, HEAD_DIM)
    total_heads = whole[:, width:packed_rows].reshape(sections, heads, HEAD_DIM)

    query_normed = layer_normalizer(query_block.astype(jnp.float32), query_gain).astype(
        jnp.bfloat16
    )
    query_feats = feature_map(
        jnp.dot(query_normed, query_weight, preferred_element_type=jnp.float32)
    ).astype(jnp.bfloat16)
    per_head_queries = query_feats.reshape(rows, heads, HEAD_DIM)

    joined = jnp.concatenate(
        [
            state_heads.transpose(1, 2, 0, 3).reshape(heads, HEAD_DIM, sections * HEAD_DIM),
            total_heads.transpose(1, 2, 0),
            jnp.zeros((heads, HEAD_DIM, HEAD_DIM - sections), jnp.float32),
        ],
        axis=2,
    )
    high = joined.astype(jnp.bfloat16)
    rest = joined - high.astype(jnp.float32)
    middle = rest.astype(jnp.bfloat16)
    low = (rest - middle.astype(jnp.float32)).astype(jnp.bfloat16)
    terms = jnp.concatenate([high, middle, low], axis=1)

    head_queries = per_head_queries.transpose(1, 0, 2)
    tripled = jnp.concatenate([head_queries] * 3, axis=2)
    products = jnp.einsum("hrk,hkc->hrc", tripled, terms, preferred_element_type=jnp.float32)
    numerator = products[:, :, : sections * HEAD_DIM].reshape(heads, rows, sections, HEAD_DIM)
    denom = products[:, :, sections * HEAD_DIM : sections * HEAD_DIM + sections]
    attended = jnp.sum(numerator / denom[:, :, :, None], axis=2).astype(jnp.bfloat16)
    mixed = query_block.astype(jnp.float32) + jnp.einsum(
        "hrv,hvd->rd",
        attended,
        output_weight.reshape(heads, HEAD_DIM, width),
        preferred_element_type=jnp.float32,
    )
    centred = layer_normalizer(mixed, middle_gain).astype(jnp.bfloat16)

    share = width // sections
    chunks = 2 if rows % 16 == 0 else 1
    step = rows // chunks
    outs = []
    for c in range(chunks):
        hidden = jax.nn.gelu(
            jnp.dot(centred[c * step : (c + 1) * step], up_weight, preferred_element_type=jnp.float32),
            approximate=True,
        ).astype(jnp.bfloat16)
        term = jnp.dot(hidden, down_weight, preferred_element_type=jnp.float32)
        parts = term.astype(jnp.bfloat16).reshape(step, sections, share).transpose(1, 0, 2)
        summed = jnp.sum(
            lax.all_to_all(parts, "sec", 0, 0, tiled=False).astype(jnp.float32), axis=0
        )
        own_mixed = lax.dynamic_slice_in_dim(mixed[c * step : (c + 1) * step], me * share, share, axis=1)
        outs.append((own_mixed + summed).astype(jnp.bfloat16))
    return jnp.concatenate(outs, axis=0)


def solution(mesh):
    placed = (
        P("sec", "pts", None),
        P("sec", "pts"),
        P("sec", None),
        P("sec", "pts", None),
        P("sec", "pts", None),
        P(),
        P(),
        P(),
        P(None, "sec"),
        P("sec", None),
    )
    return jax.shard_map(
        on_device, mesh=mesh, in_specs=placed, out_specs=P("pts", "sec"), check_vma=False
    )
```

```python
import jax
import jax.numpy as jnp
from jax import lax
from jax.sharding import PartitionSpec as P

HEAD_DIM = 128


def layer_normalizer(values, gain):
    mean = jnp.mean(values, axis=-1, keepdims=True)
    centred = values - mean
    spread = jnp.mean(centred * centred, axis=-1, keepdims=True)
    return centred * lax.rsqrt(spread + 1e-05) * gain


def feature_map(values):
    return jax.nn.elu(values) + 1.0


def from_last(value, axis, sections):
    me = lax.axis_index(axis)
    last = sections - 1
    if sections != 4:
        out = value
        for target in range(last):
            got = lax.ppermute(value, axis, [(last, target)])
            out = jnp.where(me == target, got, out)
        return out
    far = lax.ppermute(value, axis, [(3, 1)])
    near = lax.ppermute(value, axis, [(3, 2)])
    farther = lax.ppermute(far, axis, [(1, 0)])
    return jnp.where(
        me == 3, value, jnp.where(me == 2, near, jnp.where(me == 1, far, farther))
    )


def gather_a2a(value, axis, count):
    spread = jnp.broadcast_to(value[None], (count,) + value.shape)
    return lax.all_to_all(spread, axis, 0, 0, tiled=False)


def scatter_sum(term, me, sections):
    rows, width = term.shape
    share = width // sections
    if sections != 4:
        parts = term.astype(jnp.bfloat16).reshape(rows, sections, share).transpose(1, 0, 2)
        got = lax.all_to_all(parts, "sec", 0, 0, tiled=False)
        return jnp.sum(got.astype(jnp.float32), axis=0)
    half = width // 2
    mine = me // 2
    sent = lax.dynamic_slice_in_dim(term, (1 - mine) * half, half, axis=1)
    got = lax.ppermute(sent.astype(jnp.bfloat16), "sec", [(0, 2), (2, 0), (1, 3), (3, 1)])
    halved = lax.dynamic_slice_in_dim(term, mine * half, half, axis=1) + got.astype(jnp.float32)
    inner = me % 2
    sent = lax.dynamic_slice_in_dim(halved, (1 - inner) * share, share, axis=1)
    got = lax.ppermute(sent.astype(jnp.bfloat16), "sec", [(0, 1), (1, 0), (2, 3), (3, 2)])
    return lax.dynamic_slice_in_dim(halved, inner * share, share, axis=1) + got.astype(jnp.float32)


def on_device(
    points,
    counts,
    input_gain,
    key_weight,
    value_weight,
    query_weight,
    output_weight,
    middle_gain,
    up_weight,
    down_weight,
):
    block = points[0]
    rows = block.shape[0]
    width = block.shape[1]
    heads = width // HEAD_DIM
    sections = lax.axis_size("sec")
    blocks = lax.axis_size("pts")
    me = lax.axis_index("sec")

    stacked = jnp.concatenate([key_weight[0], value_weight[0]], axis=1)
    weights = gather_a2a(stacked, "pts", blocks).reshape(width, 2 * width)

    late_block, late_gain, weights = lax.optimization_barrier((block, input_gain[0], weights))
    query_block = from_last(late_block, "sec", sections)
    query_gain = from_last(late_gain, "sec", sections)

    normed = layer_normalizer(block.astype(jnp.float32), input_gain[0]).astype(jnp.bfloat16)
    projected = jnp.dot(normed, weights, preferred_element_type=jnp.float32)
    valid = jnp.arange(rows) < counts[0, 0]
    key_feats = feature_map(projected[:, :width]).astype(jnp.bfloat16)
    key_feats = jnp.where(valid[:, None], key_feats, jnp.zeros_like(key_feats))
    value_rows = projected[:, width:].astype(jnp.bfloat16)
    local_state = jnp.einsum(
        "yzl,yzn->zln",
        key_feats.reshape(rows, heads, HEAD_DIM),
        value_rows.reshape(rows, heads, HEAD_DIM),
        preferred_element_type=jnp.float32,
    ).reshape(width, HEAD_DIM)
    local_total = jnp.sum(key_feats.astype(jnp.float32), axis=0).reshape(heads, HEAD_DIM)

    packed_rows = width + heads
    piece = -(-packed_rows // blocks)
    packed = jnp.concatenate(
        [
            local_state,
            local_total,
            jnp.zeros((piece * blocks - packed_rows, HEAD_DIM), jnp.float32),
        ],
        axis=0,
    ).reshape(blocks, piece, HEAD_DIM)
    reduced = jnp.sum(lax.all_to_all(packed, "pts", 0, 0, tiled=False), axis=0)
    by_section = gather_a2a(reduced, "sec", sections)
    whole = gather_a2a(by_section, "pts", blocks)
    whole = whole.transpose(1, 0, 2, 3).reshape(sections, blocks * piece, HEAD_DIM)
    state_heads = whole[:, :width].reshape(sections, heads, HEAD_DIM, HEAD_DIM)
    total_heads = whole[:, width:packed_rows].reshape(sections, heads, HEAD_DIM)

    query_normed = layer_normalizer(query_block.astype(jnp.float32), query_gain).astype(
        jnp.bfloat16
    )
    query_feats = feature_map(
        jnp.dot(query_normed, query_weight, preferred_element_type=jnp.float32)
    ).astype(jnp.bfloat16)
    per_head_queries = query_feats.astype(jnp.float32).reshape(rows, heads, HEAD_DIM)
    numerator = jnp.einsum(
        "rhk,shkv->srhv", per_head_queries, state_heads, precision=lax.Precision.HIGHEST
    )
    denom = jnp.einsum(
        "rhk,shk->srh", per_head_queries, total_heads, precision=lax.Precision.HIGHEST
    )
    attended = (
        jnp.sum(numerator / denom[:, :, :, None], axis=0).reshape(rows, width).astype(jnp.bfloat16)
    )
    mixed = query_block.astype(jnp.float32) + jnp.dot(
        attended, output_weight, preferred_element_type=jnp.float32
    )
    centred = layer_normalizer(mixed, middle_gain).astype(jnp.bfloat16)
    hidden = jax.nn.gelu(
        jnp.dot(centred, up_weight, preferred_element_type=jnp.float32), approximate=True
    ).astype(jnp.bfloat16)
    term = jnp.dot(hidden, down_weight, preferred_element_type=jnp.float32)
    share = width // sections
    own_mixed = lax.dynamic_slice_in_dim(mixed, me * share, share, axis=1)
    return (own_mixed + scatter_sum(term, me, sections)).astype(jnp.bfloat16)


def solution(mesh):
    placed = (
        P("sec", "pts", None),
        P("sec", "pts"),
        P("sec", None),
        P("sec", "pts", None),
        P("sec", "pts", None),
        P(),
        P(),
        P(),
        P(None, "sec"),
        P("sec", None),
    )
    return jax.shard_map(
        on_device, mesh=mesh, in_specs=placed, out_specs=P("pts", "sec"), check_vma=False
    )
```

```python
import jax
import jax.numpy as jnp
from jax import lax
from jax.sharding import PartitionSpec as P

HEAD_DIM = 128


def layer_normalizer(values, gain):
    mean = jnp.mean(values, axis=-1, keepdims=True)
    centred = values - mean
    spread = jnp.mean(centred * centred, axis=-1, keepdims=True)
    return centred * lax.rsqrt(spread + 1e-05) * gain


def feature_map(values):
    return jax.nn.elu(values) + 1.0


def from_last(value, axis, sections):
    me = lax.axis_index(axis)
    last = sections - 1
    if sections != 4:
        out = value
        for target in range(last):
            got = lax.ppermute(value, axis, [(last, target)])
            out = jnp.where(me == target, got, out)
        return out
    far = lax.ppermute(value, axis, [(3, 1)])
    near = lax.ppermute(value, axis, [(3, 2)])
    farther = lax.ppermute(far, axis, [(1, 0)])
    return jnp.where(
        me == 3, value, jnp.where(me == 2, near, jnp.where(me == 1, far, farther))
    )


def gather_a2a(value, axis, count):
    spread = jnp.broadcast_to(value[None], (count,) + value.shape)
    return lax.all_to_all(spread, axis, 0, 0, tiled=False)


def scatter_sum(term, me, sections):
    rows, width = term.shape
    share = width // sections
    if sections != 4:
        parts = term.astype(jnp.bfloat16).reshape(rows, sections, share).transpose(1, 0, 2)
        got = lax.all_to_all(parts, "sec", 0, 0, tiled=False)
        return jnp.sum(got.astype(jnp.float32), axis=0)
    parity = me % 2
    quarters = term.reshape(rows, 2, 2, share)
    kept = lax.dynamic_index_in_dim(quarters, parity, axis=2, keepdims=False)
    sent = lax.dynamic_index_in_dim(quarters, 1 - parity, axis=2, keepdims=False)
    got = lax.ppermute(sent.astype(jnp.bfloat16), "sec", [(0, 1), (1, 0), (2, 3), (3, 2)])
    chip = kept + got.astype(jnp.float32)
    side = me // 2
    mine = lax.dynamic_index_in_dim(chip, side, axis=1, keepdims=False)
    other = lax.dynamic_index_in_dim(chip, 1 - side, axis=1, keepdims=False)
    got = lax.ppermute(other.astype(jnp.bfloat16), "sec", [(0, 2), (2, 0), (1, 3), (3, 1)])
    return mine + got.astype(jnp.float32)


def on_device(
    points,
    counts,
    input_gain,
    key_weight,
    value_weight,
    query_weight,
    output_weight,
    middle_gain,
    up_weight,
    down_weight,
):
    block = points[0]
    rows = block.shape[0]
    width = block.shape[1]
    heads = width // HEAD_DIM
    sections = lax.axis_size("sec")
    blocks = lax.axis_size("pts")
    me = lax.axis_index("sec")

    stacked = jnp.concatenate([key_weight[0], value_weight[0]], axis=1)
    weights = gather_a2a(stacked, "pts", blocks).reshape(width, 2 * width)

    late_block, late_gain, weights = lax.optimization_barrier((block, input_gain[0], weights))
    query_block = from_last(late_block, "sec", sections)
    query_gain = from_last(late_gain, "sec", sections)

    normed = layer_normalizer(block.astype(jnp.float32), input_gain[0]).astype(jnp.bfloat16)
    projected = jnp.dot(normed, weights, preferred_element_type=jnp.float32)
    valid = jnp.arange(rows) < counts[0, 0]
    key_feats = feature_map(projected[:, :width]).astype(jnp.bfloat16)
    key_feats = jnp.where(valid[:, None], key_feats, jnp.zeros_like(key_feats))
    value_rows = projected[:, width:].astype(jnp.bfloat16)
    local_state = jnp.einsum(
        "yzl,yzn->zln",
        key_feats.reshape(rows, heads, HEAD_DIM),
        value_rows.reshape(rows, heads, HEAD_DIM),
        preferred_element_type=jnp.float32,
    ).reshape(width, HEAD_DIM)
    local_total = jnp.sum(key_feats.astype(jnp.float32), axis=0).reshape(heads, HEAD_DIM)

    packed_rows = width + heads
    piece = -(-packed_rows // blocks)
    packed = jnp.concatenate(
        [
            local_state,
            local_total,
            jnp.zeros((piece * blocks - packed_rows, HEAD_DIM), jnp.float32),
        ],
        axis=0,
    ).reshape(blocks, piece, HEAD_DIM)
    reduced = jnp.sum(lax.all_to_all(packed, "pts", 0, 0, tiled=False), axis=0)
    by_section = gather_a2a(reduced, "sec", sections)
    whole = gather_a2a(by_section, "pts", blocks)
    whole = whole.transpose(1, 0, 2, 3).reshape(sections, blocks * piece, HEAD_DIM)
    state_heads = whole[:, :width].reshape(sections, heads, HEAD_DIM, HEAD_DIM)
    total_heads = whole[:, width:packed_rows].reshape(sections, heads, HEAD_DIM)

    query_normed = layer_normalizer(query_block.astype(jnp.float32), query_gain).astype(
        jnp.bfloat16
    )
    query_feats = feature_map(
        jnp.dot(query_normed, query_weight, preferred_element_type=jnp.float32)
    ).astype(jnp.bfloat16)
    per_head_queries = query_feats.astype(jnp.float32).reshape(rows, heads, HEAD_DIM)
    numerator = jnp.einsum(
        "rhk,shkv->srhv", per_head_queries, state_heads, precision=lax.Precision.HIGHEST
    )
    denom = jnp.einsum(
        "rhk,shk->srh", per_head_queries, total_heads, precision=lax.Precision.HIGHEST
    )
    attended = (
        jnp.sum(numerator / denom[:, :, :, None], axis=0).reshape(rows, width).astype(jnp.bfloat16)
    )
    mixed = query_block.astype(jnp.float32) + jnp.dot(
        attended, output_weight, preferred_element_type=jnp.float32
    )
    centred = layer_normalizer(mixed, middle_gain).astype(jnp.bfloat16)
    hidden = jax.nn.gelu(
        jnp.dot(centred, up_weight, preferred_element_type=jnp.float32), approximate=True
    ).astype(jnp.bfloat16)
    term = jnp.dot(hidden, down_weight, preferred_element_type=jnp.float32)
    share = width // sections
    own_mixed = lax.dynamic_slice_in_dim(mixed, me * share, share, axis=1)
    return (own_mixed + scatter_sum(term, me, sections)).astype(jnp.bfloat16)


def solution(mesh):
    placed = (
        P("sec", "pts", None),
        P("sec", "pts"),
        P("sec", None),
        P("sec", "pts", None),
        P("sec", "pts", None),
        P(),
        P(),
        P(),
        P(None, "sec"),
        P("sec", None),
    )
    return jax.shard_map(
        on_device, mesh=mesh, in_specs=placed, out_specs=P("pts", "sec"), check_vma=False
    )
```

```python
import jax
import jax.numpy as jnp
from jax import lax
from jax.sharding import PartitionSpec as P

HEAD_DIM = 128


def layer_normalizer(values, gain):
    mean = jnp.mean(values, axis=-1, keepdims=True)
    centred = values - mean
    spread = jnp.mean(centred * centred, axis=-1, keepdims=True)
    return centred * lax.rsqrt(spread + 1e-05) * gain


def feature_map(values):
    return jax.nn.elu(values) + 1.0


def from_last(value, axis, sections):
    me = lax.axis_index(axis)
    last = sections - 1
    if sections != 4:
        out = value
        for target in range(last):
            got = lax.ppermute(value, axis, [(last, target)])
            out = jnp.where(me == target, got, out)
        return out
    far = lax.ppermute(value, axis, [(3, 1)])
    near = lax.ppermute(value, axis, [(3, 2)])
    farther = lax.ppermute(far, axis, [(1, 0)])
    return jnp.where(
        me == 3, value, jnp.where(me == 2, near, jnp.where(me == 1, far, farther))
    )


def gather_a2a(value, axis, count):
    spread = jnp.broadcast_to(value[None], (count,) + value.shape)
    return lax.all_to_all(spread, axis, 0, 0, tiled=False)


def scatter_sum(term, me, sections):
    rows, width = term.shape
    share = width // sections
    if sections != 4:
        parts = term.astype(jnp.bfloat16).reshape(rows, sections, share).transpose(1, 0, 2)
        got = lax.all_to_all(parts, "sec", 0, 0, tiled=False)
        return jnp.sum(got.astype(jnp.float32), axis=0)
    parity = me % 2
    quarters = term.reshape(rows, 2, 2, share)
    kept = lax.dynamic_index_in_dim(quarters, parity, axis=2, keepdims=False)
    sent = lax.dynamic_index_in_dim(quarters, 1 - parity, axis=2, keepdims=False)
    got = lax.ppermute(sent.astype(jnp.bfloat16), "sec", [(0, 1), (1, 0), (2, 3), (3, 2)])
    chip = kept + got.astype(jnp.float32)
    side = me // 2
    mine = lax.dynamic_index_in_dim(chip, side, axis=1, keepdims=False)
    other = lax.dynamic_index_in_dim(chip, 1 - side, axis=1, keepdims=False)
    got = lax.ppermute(other.astype(jnp.bfloat16), "sec", [(0, 2), (2, 0), (1, 3), (3, 1)])
    return mine + got.astype(jnp.float32)


def on_device(
    points,
    counts,
    input_gain,
    key_weight,
    value_weight,
    query_weight,
    output_weight,
    middle_gain,
    up_weight,
    down_weight,
):
    block = points[0]
    rows = block.shape[0]
    width = block.shape[1]
    heads = width // HEAD_DIM
    sections = lax.axis_size("sec")
    blocks = lax.axis_size("pts")
    me = lax.axis_index("sec")

    stacked = jnp.concatenate([key_weight[0], value_weight[0]], axis=1)
    weights = gather_a2a(stacked, "pts", blocks).reshape(width, 2 * width)

    query_block = from_last(block, "sec", sections)
    query_gain = from_last(input_gain[0], "sec", sections)
    query_normed = layer_normalizer(query_block.astype(jnp.float32), query_gain).astype(
        jnp.bfloat16
    )
    query_feats = feature_map(
        jnp.dot(query_normed, query_weight, preferred_element_type=jnp.float32)
    ).astype(jnp.bfloat16)
    weights, query_feats = lax.optimization_barrier((weights, query_feats))

    normed = layer_normalizer(block.astype(jnp.float32), input_gain[0]).astype(jnp.bfloat16)
    projected = jnp.dot(normed, weights, preferred_element_type=jnp.float32)
    valid = jnp.arange(rows) < counts[0, 0]
    key_feats = feature_map(projected[:, :width]).astype(jnp.bfloat16)
    key_feats = jnp.where(valid[:, None], key_feats, jnp.zeros_like(key_feats))
    value_rows = projected[:, width:].astype(jnp.bfloat16)
    local_state = jnp.einsum(
        "yzl,yzn->zln",
        key_feats.reshape(rows, heads, HEAD_DIM),
        value_rows.reshape(rows, heads, HEAD_DIM),
        preferred_element_type=jnp.float32,
    ).reshape(width, HEAD_DIM)
    local_total = jnp.sum(key_feats.astype(jnp.float32), axis=0).reshape(heads, HEAD_DIM)

    packed_rows = width + heads
    piece = -(-packed_rows // blocks)
    packed = jnp.concatenate(
        [
            local_state,
            local_total,
            jnp.zeros((piece * blocks - packed_rows, HEAD_DIM), jnp.float32),
        ],
        axis=0,
    ).reshape(blocks, piece, HEAD_DIM)
    reduced = jnp.sum(lax.all_to_all(packed, "pts", 0, 0, tiled=False), axis=0)
    by_section = gather_a2a(reduced, "sec", sections)
    whole = gather_a2a(by_section, "pts", blocks)
    whole = whole.transpose(1, 0, 2, 3).reshape(sections, blocks * piece, HEAD_DIM)
    state_heads = whole[:, :width].reshape(sections, heads, HEAD_DIM, HEAD_DIM)
    total_heads = whole[:, width:packed_rows].reshape(sections, heads, HEAD_DIM)

    per_head_queries = query_feats.astype(jnp.float32).reshape(rows, heads, HEAD_DIM)
    numerator = jnp.einsum(
        "rhk,shkv->srhv", per_head_queries, state_heads, precision=lax.Precision.HIGH
    )
    denom = jnp.einsum(
        "rhk,shk->srh", per_head_queries, total_heads, precision=lax.Precision.HIGH
    )
    attended = (
        jnp.sum(numerator / denom[:, :, :, None], axis=0).reshape(rows, width).astype(jnp.bfloat16)
    )
    mixed = query_block.astype(jnp.float32) + jnp.dot(
        attended, output_weight, preferred_element_type=jnp.float32
    )
    centred = layer_normalizer(mixed, middle_gain).astype(jnp.bfloat16)
    hidden = jax.nn.gelu(
        jnp.dot(centred, up_weight, preferred_element_type=jnp.float32), approximate=True
    ).astype(jnp.bfloat16)
    term = jnp.dot(hidden, down_weight, preferred_element_type=jnp.float32)
    share = width // sections
    own_mixed = lax.dynamic_slice_in_dim(mixed, me * share, share, axis=1)
    return (own_mixed + scatter_sum(term, me, sections)).astype(jnp.bfloat16)


def solution(mesh):
    placed = (
        P("sec", "pts", None),
        P("sec", "pts"),
        P("sec", None),
        P("sec", "pts", None),
        P("sec", "pts", None),
        P(),
        P(),
        P(),
        P(None, "sec"),
        P("sec", None),
    )
    return jax.shard_map(
        on_device, mesh=mesh, in_specs=placed, out_specs=P("pts", "sec"), check_vma=False
    )
```

```python
import jax
import jax.numpy as jnp
from jax import lax
from jax.sharding import PartitionSpec as P

HEAD_DIM = 128


def layer_normalizer(values, gain):
    mean = jnp.mean(values, axis=-1, keepdims=True)
    centred = values - mean
    spread = jnp.mean(centred * centred, axis=-1, keepdims=True)
    return centred * lax.rsqrt(spread + 1e-05) * gain


def feature_map(values):
    return jax.nn.elu(values) + 1.0


def from_last(value, axis, sections):
    me = lax.axis_index(axis)
    last = sections - 1
    if sections != 4:
        out = value
        for target in range(last):
            got = lax.ppermute(value, axis, [(last, target)])
            out = jnp.where(me == target, got, out)
        return out
    far = lax.ppermute(value, axis, [(3, 1)])
    near = lax.ppermute(value, axis, [(3, 2)])
    farther = lax.ppermute(far, axis, [(1, 0)])
    return jnp.where(
        me == 3, value, jnp.where(me == 2, near, jnp.where(me == 1, far, farther))
    )


def gather_a2a(value, axis, count):
    spread = jnp.broadcast_to(value[None], (count,) + value.shape)
    return lax.all_to_all(spread, axis, 0, 0, tiled=False)


def scatter_sum(term, me, sections):
    rows, width = term.shape
    share = width // sections
    if sections != 4:
        parts = term.astype(jnp.bfloat16).reshape(rows, sections, share).transpose(1, 0, 2)
        got = lax.all_to_all(parts, "sec", 0, 0, tiled=False)
        return jnp.sum(got.astype(jnp.float32), axis=0)
    parity = me % 2
    quarters = term.reshape(rows, 2, 2, share)
    kept = lax.dynamic_index_in_dim(quarters, parity, axis=2, keepdims=False)
    sent = lax.dynamic_index_in_dim(quarters, 1 - parity, axis=2, keepdims=False)
    got = lax.ppermute(sent.astype(jnp.bfloat16), "sec", [(0, 1), (1, 0), (2, 3), (3, 2)])
    chip = kept + got.astype(jnp.float32)
    side = me // 2
    mine = lax.dynamic_index_in_dim(chip, side, axis=1, keepdims=False)
    other = lax.dynamic_index_in_dim(chip, 1 - side, axis=1, keepdims=False)
    got = lax.ppermute(other.astype(jnp.bfloat16), "sec", [(0, 2), (2, 0), (1, 3), (3, 1)])
    return mine + got.astype(jnp.float32)


def on_device(
    points,
    counts,
    input_gain,
    key_weight,
    value_weight,
    query_weight,
    output_weight,
    middle_gain,
    up_weight,
    down_weight,
):
    block = points[0]
    rows = block.shape[0]
    width = block.shape[1]
    heads = width // HEAD_DIM
    sections = lax.axis_size("sec")
    blocks = lax.axis_size("pts")
    me = lax.axis_index("sec")

    stacked = jnp.concatenate([key_weight[0], value_weight[0]], axis=1)
    weights = gather_a2a(stacked, "pts", blocks).reshape(width, 2 * width)

    late_block, late_gain, weights = lax.optimization_barrier((block, input_gain[0], weights))
    query_block = from_last(late_block, "sec", sections)
    query_gain = from_last(late_gain, "sec", sections)

    normed = layer_normalizer(block.astype(jnp.float32), input_gain[0]).astype(jnp.bfloat16)
    projected = jnp.dot(normed, weights, preferred_element_type=jnp.float32)
    valid = jnp.arange(rows) < counts[0, 0]
    key_feats = feature_map(projected[:, :width]).astype(jnp.bfloat16)
    key_feats = jnp.where(valid[:, None], key_feats, jnp.zeros_like(key_feats))
    value_rows = projected[:, width:].astype(jnp.bfloat16)
    local_state = jnp.einsum(
        "yzl,yzn->zln",
        key_feats.reshape(rows, heads, HEAD_DIM),
        value_rows.reshape(rows, heads, HEAD_DIM),
        preferred_element_type=jnp.float32,
    ).reshape(width, HEAD_DIM)
    local_total = jnp.sum(key_feats.astype(jnp.float32), axis=0).reshape(heads, HEAD_DIM)

    packed_rows = width + heads
    piece = -(-packed_rows // blocks)
    packed = jnp.concatenate(
        [
            local_state,
            local_total,
            jnp.zeros((piece * blocks - packed_rows, HEAD_DIM), jnp.float32),
        ],
        axis=0,
    ).reshape(blocks, piece, HEAD_DIM)
    reduced = jnp.sum(lax.all_to_all(packed, "pts", 0, 0, tiled=False), axis=0)
    by_section = gather_a2a(reduced, "sec", sections)
    whole = gather_a2a(by_section, "pts", blocks)
    whole = whole.transpose(1, 0, 2, 3).reshape(sections, blocks * piece, HEAD_DIM)
    state_heads = whole[:, :width].reshape(sections, heads, HEAD_DIM, HEAD_DIM)
    total_heads = whole[:, width:packed_rows].reshape(sections, heads, HEAD_DIM)

    query_normed = layer_normalizer(query_block.astype(jnp.float32), query_gain).astype(
        jnp.bfloat16
    )
    query_feats = feature_map(
        jnp.dot(query_normed, query_weight, preferred_element_type=jnp.float32)
    ).astype(jnp.bfloat16)
    per_head_queries = query_feats.astype(jnp.float32).reshape(rows, heads, HEAD_DIM)
    numerator = jnp.einsum(
        "rhk,shkv->srhv", per_head_queries, state_heads, precision=lax.Precision.HIGH
    )
    denom = jnp.einsum(
        "rhk,shk->srh", per_head_queries, total_heads, precision=lax.Precision.HIGH
    )
    attended = (
        jnp.sum(numerator / denom[:, :, :, None], axis=0).reshape(rows, width).astype(jnp.bfloat16)
    )
    mixed = query_block.astype(jnp.float32) + jnp.dot(
        attended, output_weight, preferred_element_type=jnp.float32
    )
    centred = layer_normalizer(mixed, middle_gain).astype(jnp.bfloat16)
    hidden = jax.nn.gelu(
        jnp.dot(centred, up_weight, preferred_element_type=jnp.float32), approximate=True
    ).astype(jnp.bfloat16)
    term = jnp.dot(hidden, down_weight, preferred_element_type=jnp.float32)
    share = width // sections
    own_mixed = lax.dynamic_slice_in_dim(mixed, me * share, share, axis=1)
    return (own_mixed + scatter_sum(term, me, sections)).astype(jnp.bfloat16)


def solution(mesh):
    placed = (
        P("sec", "pts", None),
        P("sec", "pts"),
        P("sec", None),
        P("sec", "pts", None),
        P("sec", "pts", None),
        P(),
        P(),
        P(),
        P(None, "sec"),
        P("sec", None),
    )
    return jax.shard_map(
        on_device, mesh=mesh, in_specs=placed, out_specs=P("pts", "sec"), check_vma=False
    )
```

```python
import jax
import jax.numpy as jnp
from jax import lax
from jax.sharding import PartitionSpec as P

HEAD_DIM = 128


def layer_normalizer(values, gain):
    mean = jnp.mean(values, axis=-1, keepdims=True)
    centred = values - mean
    spread = jnp.mean(centred * centred, axis=-1, keepdims=True)
    return centred * lax.rsqrt(spread + 1e-05) * gain


def feature_map(values):
    return jax.nn.elu(values) + 1.0


def from_last(value, axis, sections):
    me = lax.axis_index(axis)
    last = sections - 1
    if sections != 4:
        out = value
        for target in range(last):
            got = lax.ppermute(value, axis, [(last, target)])
            out = jnp.where(me == target, got, out)
        return out
    far = lax.ppermute(value, axis, [(3, 1)])
    near = lax.ppermute(value, axis, [(3, 2)])
    farther = lax.ppermute(far, axis, [(1, 0)])
    return jnp.where(
        me == 3, value, jnp.where(me == 2, near, jnp.where(me == 1, far, farther))
    )


def gather_a2a(value, axis, count):
    spread = jnp.broadcast_to(value[None], (count,) + value.shape)
    return lax.all_to_all(spread, axis, 0, 0, tiled=False)


def scatter_sum(term, me, sections):
    rows, width = term.shape
    share = width // sections
    if sections != 4:
        parts = term.astype(jnp.bfloat16).reshape(rows, sections, share).transpose(1, 0, 2)
        got = lax.all_to_all(parts, "sec", 0, 0, tiled=False)
        return jnp.sum(got.astype(jnp.float32), axis=0)
    parity = me % 2
    quarters = term.reshape(rows, 2, 2, share)
    kept = lax.dynamic_index_in_dim(quarters, parity, axis=2, keepdims=False)
    sent = lax.dynamic_index_in_dim(quarters, 1 - parity, axis=2, keepdims=False)
    got = lax.ppermute(sent.astype(jnp.bfloat16), "sec", [(0, 1), (1, 0), (2, 3), (3, 2)])
    chip = kept + got.astype(jnp.float32)
    side = me // 2
    mine = lax.dynamic_index_in_dim(chip, side, axis=1, keepdims=False)
    other = lax.dynamic_index_in_dim(chip, 1 - side, axis=1, keepdims=False)
    got = lax.ppermute(other.astype(jnp.bfloat16), "sec", [(0, 2), (2, 0), (1, 3), (3, 1)])
    return mine + got.astype(jnp.float32)


def on_device(
    points,
    counts,
    input_gain,
    key_weight,
    value_weight,
    query_weight,
    output_weight,
    middle_gain,
    up_weight,
    down_weight,
):
    block = points[0]
    rows = block.shape[0]
    width = block.shape[1]
    heads = width // HEAD_DIM
    sections = lax.axis_size("sec")
    blocks = lax.axis_size("pts")
    me = lax.axis_index("sec")

    stacked = jnp.concatenate([key_weight[0], value_weight[0]], axis=1)
    weights = gather_a2a(stacked, "pts", blocks).reshape(width, 2 * width)

    late_block, late_gain, weights = lax.optimization_barrier((block, input_gain[0], weights))
    query_block = from_last(late_block, "sec", sections)
    query_gain = from_last(late_gain, "sec", sections)

    normed = layer_normalizer(block.astype(jnp.float32), input_gain[0]).astype(jnp.bfloat16)
    projected = jnp.dot(normed, weights, preferred_element_type=jnp.float32)
    valid = jnp.arange(rows) < counts[0, 0]
    key_feats = feature_map(projected[:, :width]).astype(jnp.bfloat16)
    key_feats = jnp.where(valid[:, None], key_feats, jnp.zeros_like(key_feats))
    value_rows = projected[:, width:].astype(jnp.bfloat16)
    local_state = jnp.einsum(
        "yzl,yzn->zln",
        key_feats.reshape(rows, heads, HEAD_DIM),
        value_rows.reshape(rows, heads, HEAD_DIM),
        preferred_element_type=jnp.float32,
    ).reshape(width, HEAD_DIM)
    local_total = jnp.sum(key_feats.astype(jnp.float32), axis=0).reshape(heads, HEAD_DIM)

    packed_rows = width + heads
    piece = -(-packed_rows // blocks)
    packed = jnp.concatenate(
        [
            local_state,
            local_total,
            jnp.zeros((piece * blocks - packed_rows, HEAD_DIM), jnp.float32),
        ],
        axis=0,
    ).reshape(blocks, piece, HEAD_DIM)
    reduced = jnp.sum(lax.all_to_all(packed, "pts", 0, 0, tiled=False), axis=0)
    by_section = gather_a2a(reduced.astype(jnp.bfloat16), "sec", sections)
    whole = gather_a2a(by_section, "pts", blocks).astype(jnp.float32)
    whole = whole.transpose(1, 0, 2, 3).reshape(sections, blocks * piece, HEAD_DIM)
    state_heads = whole[:, :width].reshape(sections, heads, HEAD_DIM, HEAD_DIM)
    total_heads = whole[:, width:packed_rows].reshape(sections, heads, HEAD_DIM)

    query_normed = layer_normalizer(query_block.astype(jnp.float32), query_gain).astype(
        jnp.bfloat16
    )
    query_feats = feature_map(
        jnp.dot(query_normed, query_weight, preferred_element_type=jnp.float32)
    ).astype(jnp.bfloat16)
    per_head_queries = query_feats.astype(jnp.float32).reshape(rows, heads, HEAD_DIM)
    numerator = jnp.einsum(
        "rhk,shkv->srhv", per_head_queries, state_heads, precision=lax.Precision.HIGH
    )
    denom = jnp.einsum(
        "rhk,shk->srh", per_head_queries, total_heads, precision=lax.Precision.HIGH
    )
    attended = (
        jnp.sum(numerator / denom[:, :, :, None], axis=0).reshape(rows, width).astype(jnp.bfloat16)
    )
    mixed = query_block.astype(jnp.float32) + jnp.dot(
        attended, output_weight, preferred_element_type=jnp.float32
    )
    centred = layer_normalizer(mixed, middle_gain).astype(jnp.bfloat16)
    hidden = jax.nn.gelu(
        jnp.dot(centred, up_weight, preferred_element_type=jnp.float32), approximate=True
    ).astype(jnp.bfloat16)
    term = jnp.dot(hidden, down_weight, preferred_element_type=jnp.float32)
    share = width // sections
    own_mixed = lax.dynamic_slice_in_dim(mixed, me * share, share, axis=1)
    return (own_mixed + scatter_sum(term, me, sections)).astype(jnp.bfloat16)


def solution(mesh):
    placed = (
        P("sec", "pts", None),
        P("sec", "pts"),
        P("sec", None),
        P("sec", "pts", None),
        P("sec", "pts", None),
        P(),
        P(),
        P(),
        P(None, "sec"),
        P("sec", None),
    )
    return jax.shard_map(
        on_device, mesh=mesh, in_specs=placed, out_specs=P("pts", "sec"), check_vma=False
    )
```

```python
import jax
import jax.numpy as jnp
from jax import lax
from jax.sharding import PartitionSpec as P

HEAD_DIM = 128


def layer_normalizer(values, gain):
    mean = jnp.mean(values, axis=-1, keepdims=True)
    centred = values - mean
    spread = jnp.mean(centred * centred, axis=-1, keepdims=True)
    return centred * lax.rsqrt(spread + 1e-05) * gain


def feature_map(values):
    return jax.nn.elu(values) + 1.0


def from_last(value, axis, sections):
    me = lax.axis_index(axis)
    last = sections - 1
    if sections != 4:
        out = value
        for target in range(last):
            got = lax.ppermute(value, axis, [(last, target)])
            out = jnp.where(me == target, got, out)
        return out
    far = lax.ppermute(value, axis, [(3, 1)])
    near = lax.ppermute(value, axis, [(3, 2)])
    farther = lax.ppermute(far, axis, [(1, 0)])
    return jnp.where(
        me == 3, value, jnp.where(me == 2, near, jnp.where(me == 1, far, farther))
    )


def gather_a2a(value, axis, count):
    spread = jnp.broadcast_to(value[None], (count,) + value.shape)
    return lax.all_to_all(spread, axis, 0, 0, tiled=False)


def gather_sec(value, me, sections):
    if sections != 4:
        return gather_a2a(value, "sec", sections)
    got = lax.ppermute(value, "sec", [(0, 1), (1, 0), (2, 3), (3, 2)])
    first = me % 2 == 0
    pair = jnp.where(first, jnp.stack([value, got]), jnp.stack([got, value]))
    other = lax.ppermute(pair, "sec", [(0, 2), (2, 0), (1, 3), (3, 1)])
    lower = me // 2 == 0
    return jnp.where(lower, jnp.concatenate([pair, other]), jnp.concatenate([other, pair]))


def scatter_sum(term, me, sections):
    rows, width = term.shape
    share = width // sections
    if sections != 4:
        parts = term.astype(jnp.bfloat16).reshape(rows, sections, share).transpose(1, 0, 2)
        got = lax.all_to_all(parts, "sec", 0, 0, tiled=False)
        return jnp.sum(got.astype(jnp.float32), axis=0)
    parity = me % 2
    quarters = term.reshape(rows, 2, 2, share)
    kept = lax.dynamic_index_in_dim(quarters, parity, axis=2, keepdims=False)
    sent = lax.dynamic_index_in_dim(quarters, 1 - parity, axis=2, keepdims=False)
    got = lax.ppermute(sent.astype(jnp.bfloat16), "sec", [(0, 1), (1, 0), (2, 3), (3, 2)])
    chip = kept + got.astype(jnp.float32)
    side = me // 2
    mine = lax.dynamic_index_in_dim(chip, side, axis=1, keepdims=False)
    other = lax.dynamic_index_in_dim(chip, 1 - side, axis=1, keepdims=False)
    got = lax.ppermute(other.astype(jnp.bfloat16), "sec", [(0, 2), (2, 0), (1, 3), (3, 1)])
    return mine + got.astype(jnp.float32)


def on_device(
    points,
    counts,
    input_gain,
    key_weight,
    value_weight,
    query_weight,
    output_weight,
    middle_gain,
    up_weight,
    down_weight,
):
    block = points[0]
    rows = block.shape[0]
    width = block.shape[1]
    heads = width // HEAD_DIM
    sections = lax.axis_size("sec")
    blocks = lax.axis_size("pts")
    me = lax.axis_index("sec")

    stacked = jnp.concatenate([key_weight[0], value_weight[0]], axis=1)
    weights = gather_a2a(stacked, "pts", blocks).reshape(width, 2 * width)

    late_block, late_gain, weights = lax.optimization_barrier((block, input_gain[0], weights))
    query_block = from_last(late_block, "sec", sections)
    query_gain = from_last(late_gain, "sec", sections)

    normed = layer_normalizer(block.astype(jnp.float32), input_gain[0]).astype(jnp.bfloat16)
    projected = jnp.dot(normed, weights, preferred_element_type=jnp.float32)
    valid = jnp.arange(rows) < counts[0, 0]
    key_feats = feature_map(projected[:, :width]).astype(jnp.bfloat16)
    key_feats = jnp.where(valid[:, None], key_feats, jnp.zeros_like(key_feats))
    value_rows = projected[:, width:].astype(jnp.bfloat16)
    local_state = jnp.einsum(
        "yzl,yzn->zln",
        key_feats.reshape(rows, heads, HEAD_DIM),
        value_rows.reshape(rows, heads, HEAD_DIM),
        preferred_element_type=jnp.float32,
    ).reshape(width, HEAD_DIM)
    local_total = jnp.sum(key_feats.astype(jnp.float32), axis=0).reshape(heads, HEAD_DIM)

    packed_rows = width + heads
    piece = -(-packed_rows // blocks)
    packed = jnp.concatenate(
        [
            local_state,
            local_total,
            jnp.zeros((piece * blocks - packed_rows, HEAD_DIM), jnp.float32),
        ],
        axis=0,
    ).reshape(blocks, piece, HEAD_DIM)
    reduced = jnp.sum(lax.all_to_all(packed, "pts", 0, 0, tiled=False), axis=0)
    by_section = gather_sec(reduced.astype(jnp.bfloat16), me, sections)
    whole = gather_a2a(by_section, "pts", blocks).astype(jnp.float32)
    whole = whole.transpose(1, 0, 2, 3).reshape(sections, blocks * piece, HEAD_DIM)
    state_heads = whole[:, :width].reshape(sections, heads, HEAD_DIM, HEAD_DIM)
    total_heads = whole[:, width:packed_rows].reshape(sections, heads, HEAD_DIM)

    query_normed = layer_normalizer(query_block.astype(jnp.float32), query_gain).astype(
        jnp.bfloat16
    )
    query_feats = feature_map(
        jnp.dot(query_normed, query_weight, preferred_element_type=jnp.float32)
    ).astype(jnp.bfloat16)
    per_head_queries = query_feats.astype(jnp.float32).reshape(rows, heads, HEAD_DIM)
    numerator = jnp.einsum(
        "rhk,shkv->srhv", per_head_queries, state_heads, precision=lax.Precision.HIGH
    )
    denom = jnp.einsum(
        "rhk,shk->srh", per_head_queries, total_heads, precision=lax.Precision.HIGH
    )
    attended = (
        jnp.sum(numerator / denom[:, :, :, None], axis=0).reshape(rows, width).astype(jnp.bfloat16)
    )
    mixed = query_block.astype(jnp.float32) + jnp.dot(
        attended, output_weight, preferred_element_type=jnp.float32
    )
    centred = layer_normalizer(mixed, middle_gain).astype(jnp.bfloat16)
    hidden = jax.nn.gelu(
        jnp.dot(centred, up_weight, preferred_element_type=jnp.float32), approximate=True
    ).astype(jnp.bfloat16)
    term = jnp.dot(hidden, down_weight, preferred_element_type=jnp.float32)
    share = width // sections
    own_mixed = lax.dynamic_slice_in_dim(mixed, me * share, share, axis=1)
    return (own_mixed + scatter_sum(term, me, sections)).astype(jnp.bfloat16)


def solution(mesh):
    placed = (
        P("sec", "pts", None),
        P("sec", "pts"),
        P("sec", None),
        P("sec", "pts", None),
        P("sec", "pts", None),
        P(),
        P(),
        P(),
        P(None, "sec"),
        P("sec", None),
    )
    return jax.shard_map(
        on_device, mesh=mesh, in_specs=placed, out_specs=P("pts", "sec"), check_vma=False
    )
```

```python
import jax
import jax.numpy as jnp
from jax import lax
from jax.sharding import PartitionSpec as P

HEAD_DIM = 128


def layer_normalizer(values, gain):
    mean = jnp.mean(values, axis=-1, keepdims=True)
    centred = values - mean
    spread = jnp.mean(centred * centred, axis=-1, keepdims=True)
    return centred * lax.rsqrt(spread + 1e-05) * gain


def feature_map(values):
    return jax.nn.elu(values) + 1.0


def from_last(value, axis, sections):
    me = lax.axis_index(axis)
    last = sections - 1
    if sections != 4:
        out = value
        for target in range(last):
            got = lax.ppermute(value, axis, [(last, target)])
            out = jnp.where(me == target, got, out)
        return out
    far = lax.ppermute(value, axis, [(3, 1)])
    near = lax.ppermute(value, axis, [(3, 2)])
    farther = lax.ppermute(far, axis, [(1, 0)])
    return jnp.where(
        me == 3, value, jnp.where(me == 2, near, jnp.where(me == 1, far, farther))
    )


def gather_a2a(value, axis, count):
    spread = jnp.broadcast_to(value[None], (count,) + value.shape)
    return lax.all_to_all(spread, axis, 0, 0, tiled=False)


def gather_sec(value, me, sections):
    if sections != 4:
        return gather_a2a(value, "sec", sections)
    got = lax.ppermute(value, "sec", [(0, 1), (1, 0), (2, 3), (3, 2)])
    first = me % 2 == 0
    pair = jnp.where(first, jnp.stack([value, got]), jnp.stack([got, value]))
    other = lax.ppermute(pair, "sec", [(0, 2), (2, 0), (1, 3), (3, 1)])
    lower = me // 2 == 0
    return jnp.where(lower, jnp.concatenate([pair, other]), jnp.concatenate([other, pair]))


def scatter_sum(term, me, sections):
    rows, width = term.shape
    share = width // sections
    if sections != 4:
        parts = term.astype(jnp.bfloat16).reshape(rows, sections, share).transpose(1, 0, 2)
        got = lax.all_to_all(parts, "sec", 0, 0, tiled=False)
        return jnp.sum(got.astype(jnp.float32), axis=0)
    parity = me % 2
    quarters = term.reshape(rows, 2, 2, share)
    kept = lax.dynamic_index_in_dim(quarters, parity, axis=2, keepdims=False)
    sent = lax.dynamic_index_in_dim(quarters, 1 - parity, axis=2, keepdims=False)
    got = lax.ppermute(sent.astype(jnp.bfloat16), "sec", [(0, 1), (1, 0), (2, 3), (3, 2)])
    chip = kept + got.astype(jnp.float32)
    side = me // 2
    mine = lax.dynamic_index_in_dim(chip, side, axis=1, keepdims=False)
    other = lax.dynamic_index_in_dim(chip, 1 - side, axis=1, keepdims=False)
    got = lax.ppermute(other.astype(jnp.bfloat16), "sec", [(0, 2), (2, 0), (1, 3), (3, 1)])
    return mine + got.astype(jnp.float32)


def on_device(
    points,
    counts,
    input_gain,
    key_weight,
    value_weight,
    query_weight,
    output_weight,
    middle_gain,
    up_weight,
    down_weight,
):
    block = points[0]
    rows = block.shape[0]
    width = block.shape[1]
    heads = width // HEAD_DIM
    sections = lax.axis_size("sec")
    blocks = lax.axis_size("pts")
    me = lax.axis_index("sec")

    stacked = jnp.concatenate([key_weight[0], value_weight[0]], axis=1)
    weights = gather_a2a(stacked, "pts", blocks).reshape(width, 2 * width)

    normed = layer_normalizer(block.astype(jnp.float32), input_gain[0]).astype(jnp.bfloat16)
    own_feats = feature_map(
        jnp.dot(normed, query_weight, preferred_element_type=jnp.float32)
    ).astype(jnp.bfloat16)
    late, weights = lax.optimization_barrier((jnp.stack([own_feats, block]), weights))
    query_feats, query_block = from_last(late, "sec", sections)
    projected = jnp.dot(normed, weights, preferred_element_type=jnp.float32)
    valid = jnp.arange(rows) < counts[0, 0]
    key_feats = feature_map(projected[:, :width]).astype(jnp.bfloat16)
    key_feats = jnp.where(valid[:, None], key_feats, jnp.zeros_like(key_feats))
    value_rows = projected[:, width:].astype(jnp.bfloat16)
    local_state = jnp.einsum(
        "yzl,yzn->zln",
        key_feats.reshape(rows, heads, HEAD_DIM),
        value_rows.reshape(rows, heads, HEAD_DIM),
        preferred_element_type=jnp.float32,
    ).reshape(width, HEAD_DIM)
    local_total = jnp.sum(key_feats.astype(jnp.float32), axis=0).reshape(heads, HEAD_DIM)

    packed_rows = width + heads
    piece = -(-packed_rows // blocks)
    packed = jnp.concatenate(
        [
            local_state,
            local_total,
            jnp.zeros((piece * blocks - packed_rows, HEAD_DIM), jnp.float32),
        ],
        axis=0,
    ).reshape(blocks, piece, HEAD_DIM)
    reduced = jnp.sum(lax.all_to_all(packed, "pts", 0, 0, tiled=False), axis=0)
    by_section = gather_sec(reduced.astype(jnp.bfloat16), me, sections)
    whole = gather_a2a(by_section, "pts", blocks).astype(jnp.float32)
    whole = whole.transpose(1, 0, 2, 3).reshape(sections, blocks * piece, HEAD_DIM)
    state_heads = whole[:, :width].reshape(sections, heads, HEAD_DIM, HEAD_DIM)
    total_heads = whole[:, width:packed_rows].reshape(sections, heads, HEAD_DIM)

    per_head_queries = query_feats.astype(jnp.float32).reshape(rows, heads, HEAD_DIM)
    numerator = jnp.einsum(
        "rhk,shkv->srhv", per_head_queries, state_heads, precision=lax.Precision.HIGH
    )
    denom = jnp.einsum(
        "rhk,shk->srh", per_head_queries, total_heads, precision=lax.Precision.HIGH
    )
    attended = (
        jnp.sum(numerator / denom[:, :, :, None], axis=0).reshape(rows, width).astype(jnp.bfloat16)
    )
    mixed = query_block.astype(jnp.float32) + jnp.dot(
        attended, output_weight, preferred_element_type=jnp.float32
    )
    centred = layer_normalizer(mixed, middle_gain).astype(jnp.bfloat16)
    hidden = jax.nn.gelu(
        jnp.dot(centred, up_weight, preferred_element_type=jnp.float32), approximate=True
    ).astype(jnp.bfloat16)
    term = jnp.dot(hidden, down_weight, preferred_element_type=jnp.float32)
    share = width // sections
    own_mixed = lax.dynamic_slice_in_dim(mixed, me * share, share, axis=1)
    return (own_mixed + scatter_sum(term, me, sections)).astype(jnp.bfloat16)


def solution(mesh):
    placed = (
        P("sec", "pts", None),
        P("sec", "pts"),
        P("sec", None),
        P("sec", "pts", None),
        P("sec", "pts", None),
        P(),
        P(),
        P(),
        P(None, "sec"),
        P("sec", None),
    )
    return jax.shard_map(
        on_device, mesh=mesh, in_specs=placed, out_specs=P("pts", "sec"), check_vma=False
    )
```

```python
import jax
import jax.numpy as jnp
from jax import lax
from jax.sharding import PartitionSpec as P

HEAD_DIM = 128


def layer_normalizer(values, gain):
    mean = jnp.mean(values, axis=-1, keepdims=True)
    centred = values - mean
    spread = jnp.mean(centred * centred, axis=-1, keepdims=True)
    return centred * lax.rsqrt(spread + 1e-05) * gain


def feature_map(values):
    return jax.nn.elu(values) + 1.0


def from_last(value, axis, sections):
    me = lax.axis_index(axis)
    last = sections - 1
    if sections != 4:
        out = value
        for target in range(last):
            got = lax.ppermute(value, axis, [(last, target)])
            out = jnp.where(me == target, got, out)
        return out
    far = lax.ppermute(value, axis, [(3, 1)])
    near = lax.ppermute(value, axis, [(3, 2)])
    farther = lax.ppermute(far, axis, [(1, 0)])
    return jnp.where(
        me == 3, value, jnp.where(me == 2, near, jnp.where(me == 1, far, farther))
    )


def gather_a2a(value, axis, count):
    spread = jnp.broadcast_to(value[None], (count,) + value.shape)
    return lax.all_to_all(spread, axis, 0, 0, tiled=False)


def gather_sec(value, me, sections):
    if sections != 4:
        return gather_a2a(value, "sec", sections)
    got = lax.ppermute(value, "sec", [(0, 1), (1, 0), (2, 3), (3, 2)])
    first = me % 2 == 0
    pair = jnp.where(first, jnp.stack([value, got]), jnp.stack([got, value]))
    other = lax.ppermute(pair, "sec", [(0, 2), (2, 0), (1, 3), (3, 1)])
    lower = me // 2 == 0
    return jnp.where(lower, jnp.concatenate([pair, other]), jnp.concatenate([other, pair]))


def scatter_sum(term, me, sections):
    rows, width = term.shape
    share = width // sections
    if sections != 4:
        parts = term.astype(jnp.bfloat16).reshape(rows, sections, share).transpose(1, 0, 2)
        got = lax.all_to_all(parts, "sec", 0, 0, tiled=False)
        return jnp.sum(got.astype(jnp.float32), axis=0)
    parity = me % 2
    quarters = term.reshape(rows, 2, 2, share)
    kept = lax.dynamic_index_in_dim(quarters, parity, axis=2, keepdims=False)
    sent = lax.dynamic_index_in_dim(quarters, 1 - parity, axis=2, keepdims=False)
    got = lax.ppermute(sent.astype(jnp.bfloat16), "sec", [(0, 1), (1, 0), (2, 3), (3, 2)])
    chip = kept + got.astype(jnp.float32)
    side = me // 2
    mine = lax.dynamic_index_in_dim(chip, side, axis=1, keepdims=False)
    other = lax.dynamic_index_in_dim(chip, 1 - side, axis=1, keepdims=False)
    got = lax.ppermute(other.astype(jnp.bfloat16), "sec", [(0, 2), (2, 0), (1, 3), (3, 1)])
    return mine + got.astype(jnp.float32)


def on_device(
    points,
    counts,
    input_gain,
    key_weight,
    value_weight,
    query_weight,
    output_weight,
    middle_gain,
    up_weight,
    down_weight,
):
    block = points[0]
    rows = block.shape[0]
    width = block.shape[1]
    heads = width // HEAD_DIM
    sections = lax.axis_size("sec")
    blocks = lax.axis_size("pts")
    me = lax.axis_index("sec")

    stacked = jnp.concatenate([key_weight[0], value_weight[0]], axis=1)
    weights = gather_a2a(stacked, "pts", blocks).reshape(width, 2 * width)

    query_gain = from_last(input_gain[0], "sec", sections)
    late_block, weights = lax.optimization_barrier((block, weights))
    query_block = from_last(late_block, "sec", sections)

    normed = layer_normalizer(block.astype(jnp.float32), input_gain[0]).astype(jnp.bfloat16)
    projected = jnp.dot(normed, weights, preferred_element_type=jnp.float32)
    valid = jnp.arange(rows) < counts[0, 0]
    key_feats = feature_map(projected[:, :width]).astype(jnp.bfloat16)
    key_feats = jnp.where(valid[:, None], key_feats, jnp.zeros_like(key_feats))
    value_rows = projected[:, width:].astype(jnp.bfloat16)
    local_state = jnp.einsum(
        "yzl,yzn->zln",
        key_feats.reshape(rows, heads, HEAD_DIM),
        value_rows.reshape(rows, heads, HEAD_DIM),
        preferred_element_type=jnp.float32,
    ).reshape(width, HEAD_DIM)
    local_total = jnp.sum(key_feats.astype(jnp.float32), axis=0).reshape(heads, HEAD_DIM)

    packed_rows = width + heads
    piece = -(-packed_rows // blocks)
    packed = jnp.concatenate(
        [
            local_state,
            local_total,
            jnp.zeros((piece * blocks - packed_rows, HEAD_DIM), jnp.float32),
        ],
        axis=0,
    ).reshape(blocks, piece, HEAD_DIM)
    packed, query_block, query_gain = lax.optimization_barrier((packed, query_block, query_gain))
    reduced = jnp.sum(lax.all_to_all(packed, "pts", 0, 0, tiled=False), axis=0)
    by_section = gather_sec(reduced.astype(jnp.bfloat16), me, sections)
    whole = gather_a2a(by_section, "pts", blocks).astype(jnp.float32)
    whole = whole.transpose(1, 0, 2, 3).reshape(sections, blocks * piece, HEAD_DIM)
    state_heads = whole[:, :width].reshape(sections, heads, HEAD_DIM, HEAD_DIM)
    total_heads = whole[:, width:packed_rows].reshape(sections, heads, HEAD_DIM)

    query_normed = layer_normalizer(query_block.astype(jnp.float32), query_gain).astype(
        jnp.bfloat16
    )
    query_feats = feature_map(
        jnp.dot(query_normed, query_weight, preferred_element_type=jnp.float32)
    ).astype(jnp.bfloat16)
    per_head_queries = query_feats.astype(jnp.float32).reshape(rows, heads, HEAD_DIM)
    numerator = jnp.einsum(
        "rhk,shkv->srhv", per_head_queries, state_heads, precision=lax.Precision.HIGH
    )
    denom = jnp.einsum(
        "rhk,shk->srh", per_head_queries, total_heads, precision=lax.Precision.HIGH
    )
    attended = (
        jnp.sum(numerator / denom[:, :, :, None], axis=0).reshape(rows, width).astype(jnp.bfloat16)
    )
    mixed = query_block.astype(jnp.float32) + jnp.dot(
        attended, output_weight, preferred_element_type=jnp.float32
    )
    centred = layer_normalizer(mixed, middle_gain).astype(jnp.bfloat16)
    hidden = jax.nn.gelu(
        jnp.dot(centred, up_weight, preferred_element_type=jnp.float32), approximate=True
    ).astype(jnp.bfloat16)
    term = jnp.dot(hidden, down_weight, preferred_element_type=jnp.float32)
    share = width // sections
    own_mixed = lax.dynamic_slice_in_dim(mixed, me * share, share, axis=1)
    return (own_mixed + scatter_sum(term, me, sections)).astype(jnp.bfloat16)


def solution(mesh):
    placed = (
        P("sec", "pts", None),
        P("sec", "pts"),
        P("sec", None),
        P("sec", "pts", None),
        P("sec", "pts", None),
        P(),
        P(),
        P(),
        P(None, "sec"),
        P("sec", None),
    )

    return jax.shard_map(
        on_device, mesh=mesh, in_specs=placed, out_specs=P("pts", "sec"), check_vma=False
    )
```

```python
import jax
import jax.numpy as jnp
from jax import lax
from jax.sharding import PartitionSpec as P

HEAD_DIM = 128


def layer_normalizer(values, gain):
    mean = jnp.mean(values, axis=-1, keepdims=True)
    centred = values - mean
    spread = jnp.mean(centred * centred, axis=-1, keepdims=True)
    return centred * lax.rsqrt(spread + 1e-05) * gain


def feature_map(values):
    return jax.nn.elu(values) + 1.0


def from_last(value, axis, sections):
    me = lax.axis_index(axis)
    last = sections - 1
    if sections != 4:
        out = value
        for target in range(last):
            got = lax.ppermute(value, axis, [(last, target)])
            out = jnp.where(me == target, got, out)
        return out
    far = lax.ppermute(value, axis, [(3, 1)])
    near = lax.ppermute(value, axis, [(3, 2)])
    farther = lax.ppermute(far, axis, [(1, 0)])
    return jnp.where(
        me == 3, value, jnp.where(me == 2, near, jnp.where(me == 1, far, farther))
    )


def gather_a2a(value, axis, count):
    spread = jnp.broadcast_to(value[None], (count,) + value.shape)
    return lax.all_to_all(spread, axis, 0, 0, tiled=False)


def gather_sec(value, me, sections):
    if sections != 4:
        return gather_a2a(value, "sec", sections)
    got = lax.ppermute(value, "sec", [(0, 1), (1, 0), (2, 3), (3, 2)])
    first = me % 2 == 0
    pair = jnp.where(first, jnp.stack([value, got]), jnp.stack([got, value]))
    other = lax.ppermute(pair, "sec", [(0, 2), (2, 0), (1, 3), (3, 1)])
    lower = me // 2 == 0
    return jnp.where(lower, jnp.concatenate([pair, other]), jnp.concatenate([other, pair]))


def scatter_sum(term, me, sections):
    rows, width = term.shape
    share = width // sections
    if sections != 4:
        parts = term.astype(jnp.bfloat16).reshape(rows, sections, share).transpose(1, 0, 2)
        got = lax.all_to_all(parts, "sec", 0, 0, tiled=False)
        return jnp.sum(got.astype(jnp.float32), axis=0)
    parity = me % 2
    quarters = term.reshape(rows, 2, 2, share)
    kept = lax.dynamic_index_in_dim(quarters, parity, axis=2, keepdims=False)
    sent = lax.dynamic_index_in_dim(quarters, 1 - parity, axis=2, keepdims=False)
    got = lax.ppermute(sent.astype(jnp.bfloat16), "sec", [(0, 1), (1, 0), (2, 3), (3, 2)])
    chip = kept + got.astype(jnp.float32)
    side = me // 2
    mine = lax.dynamic_index_in_dim(chip, side, axis=1, keepdims=False)
    other = lax.dynamic_index_in_dim(chip, 1 - side, axis=1, keepdims=False)
    got = lax.ppermute(other.astype(jnp.bfloat16), "sec", [(0, 2), (2, 0), (1, 3), (3, 1)])
    return mine + got.astype(jnp.float32)


def on_device(
    points,
    counts,
    input_gain,
    key_weight,
    value_weight,
    query_weight,
    output_weight,
    middle_gain,
    up_weight,
    down_weight,
):
    block = points[0]
    rows = block.shape[0]
    width = block.shape[1]
    heads = width // HEAD_DIM
    sections = lax.axis_size("sec")
    blocks = lax.axis_size("pts")
    me = lax.axis_index("sec")

    stacked = jnp.concatenate([key_weight[0], value_weight[0]], axis=1)
    weights = gather_a2a(stacked, "pts", blocks).reshape(width, 2 * width)

    late_block, late_gain, weights = lax.optimization_barrier((block, input_gain[0], weights))
    query_block = from_last(late_block, "sec", sections)
    query_gain = from_last(late_gain, "sec", sections)

    normed = layer_normalizer(block.astype(jnp.float32), input_gain[0]).astype(jnp.bfloat16)
    projected = jnp.dot(normed, weights, preferred_element_type=jnp.float32)
    valid = jnp.arange(rows) < counts[0, 0]
    key_feats = feature_map(projected[:, :width]).astype(jnp.bfloat16)
    key_feats = jnp.where(valid[:, None], key_feats, jnp.zeros_like(key_feats))
    value_rows = projected[:, width:].astype(jnp.bfloat16)
    crossed = lax.dot_general(
        key_feats, value_rows, (((0,), (0,)), ((), ())), preferred_element_type=jnp.float32
    )
    local_state = jnp.concatenate(
        [
            crossed[h * HEAD_DIM : (h + 1) * HEAD_DIM, h * HEAD_DIM : (h + 1) * HEAD_DIM]
            for h in range(heads)
        ],
        axis=0,
    )
    local_total = jnp.sum(key_feats.astype(jnp.float32), axis=0).reshape(heads, HEAD_DIM)

    packed_rows = width + heads
    piece = -(-packed_rows // blocks)
    packed = jnp.concatenate(
        [
            local_state,
            local_total,
            jnp.zeros((piece * blocks - packed_rows, HEAD_DIM), jnp.float32),
        ],
        axis=0,
    ).reshape(blocks, piece, HEAD_DIM)
    reduced = jnp.sum(lax.all_to_all(packed, "pts", 0, 0, tiled=False), axis=0)
    by_section = gather_sec(reduced.astype(jnp.bfloat16), me, sections)
    whole = gather_a2a(by_section, "pts", blocks).astype(jnp.float32)
    whole = whole.transpose(1, 0, 2, 3).reshape(sections, blocks * piece, HEAD_DIM)
    state_heads = whole[:, :width].reshape(sections, heads, HEAD_DIM, HEAD_DIM)
    total_heads = whole[:, width:packed_rows].reshape(sections, heads, HEAD_DIM)

    query_normed = layer_normalizer(query_block.astype(jnp.float32), query_gain).astype(
        jnp.bfloat16
    )
    query_feats = feature_map(
        jnp.dot(query_normed, query_weight, preferred_element_type=jnp.float32)
    ).astype(jnp.bfloat16)
    per_head_queries = query_feats.astype(jnp.float32).reshape(rows, heads, HEAD_DIM)
    numerator = jnp.einsum(
        "rhk,shkv->srhv", per_head_queries, state_heads, precision=lax.Precision.HIGH
    )
    denom = jnp.einsum(
        "rhk,shk->srh", per_head_queries, total_heads, precision=lax.Precision.HIGH
    )
    attended = (
        jnp.sum(numerator / denom[:, :, :, None], axis=0).reshape(rows, width).astype(jnp.bfloat16)
    )
    mixed = query_block.astype(jnp.float32) + jnp.dot(
        attended, output_weight, preferred_element_type=jnp.float32
    )
    centred = layer_normalizer(mixed, middle_gain).astype(jnp.bfloat16)
    hidden = jax.nn.gelu(
        jnp.dot(centred, up_weight, preferred_element_type=jnp.float32), approximate=True
    ).astype(jnp.bfloat16)
    term = jnp.dot(hidden, down_weight, preferred_element_type=jnp.float32)
    share = width // sections
    own_mixed = lax.dynamic_slice_in_dim(mixed, me * share, share, axis=1)
    return (own_mixed + scatter_sum(term, me, sections)).astype(jnp.bfloat16)


def solution(mesh):
    placed = (
        P("sec", "pts", None),
        P("sec", "pts"),
        P("sec", None),
        P("sec", "pts", None),
        P("sec", "pts", None),
        P(),
        P(),
        P(),
        P(None, "sec"),
        P("sec", None),
    )
    return jax.shard_map(
        on_device, mesh=mesh, in_specs=placed, out_specs=P("pts", "sec"), check_vma=False
    )
```

```python
import jax
import jax.numpy as jnp
from jax import lax
from jax.sharding import PartitionSpec as P

HEAD_DIM = 128


def layer_normalizer(values, gain):
    mean = jnp.mean(values, axis=-1, keepdims=True)
    centred = values - mean
    spread = jnp.mean(centred * centred, axis=-1, keepdims=True)
    return centred * lax.rsqrt(spread + 1e-05) * gain


def feature_map(values):
    return jax.nn.elu(values) + 1.0


def from_last(value, axis, sections):
    me = lax.axis_index(axis)
    last = sections - 1
    if sections != 4:
        out = value
        for target in range(last):
            got = lax.ppermute(value, axis, [(last, target)])
            out = jnp.where(me == target, got, out)
        return out
    far = lax.ppermute(value, axis, [(3, 1)])
    near = lax.ppermute(value, axis, [(3, 2)])
    farther = lax.ppermute(far, axis, [(1, 0)])
    return jnp.where(
        me == 3, value, jnp.where(me == 2, near, jnp.where(me == 1, far, farther))
    )


def gather_a2a(value, axis, count):
    spread = jnp.broadcast_to(value[None], (count,) + value.shape)
    return lax.all_to_all(spread, axis, 0, 0, tiled=False)


def gather_sec(value, me, sections):
    if sections != 4:
        return gather_a2a(value, "sec", sections)
    got = lax.ppermute(value, "sec", [(0, 1), (1, 0), (2, 3), (3, 2)])
    first = me % 2 == 0
    pair = jnp.where(first, jnp.stack([value, got]), jnp.stack([got, value]))
    other = lax.ppermute(pair, "sec", [(0, 2), (2, 0), (1, 3), (3, 1)])
    lower = me // 2 == 0
    return jnp.where(lower, jnp.concatenate([pair, other]), jnp.concatenate([other, pair]))


def scatter_sum(term, me, sections):
    rows, width = term.shape
    share = width // sections
    if sections != 4:
        parts = term.astype(jnp.bfloat16).reshape(rows, sections, share).transpose(1, 0, 2)
        got = lax.all_to_all(parts, "sec", 0, 0, tiled=False)
        return jnp.sum(got.astype(jnp.float32), axis=0)
    parity = me % 2
    quarters = term.reshape(rows, 2, 2, share)
    kept = lax.dynamic_index_in_dim(quarters, parity, axis=2, keepdims=False)
    sent = lax.dynamic_index_in_dim(quarters, 1 - parity, axis=2, keepdims=False)
    got = lax.ppermute(sent.astype(jnp.bfloat16), "sec", [(0, 1), (1, 0), (2, 3), (3, 2)])
    chip = kept + got.astype(jnp.float32)
    side = me // 2
    mine = lax.dynamic_index_in_dim(chip, side, axis=1, keepdims=False)
    other = lax.dynamic_index_in_dim(chip, 1 - side, axis=1, keepdims=False)
    got = lax.ppermute(other.astype(jnp.bfloat16), "sec", [(0, 2), (2, 0), (1, 3), (3, 1)])
    return mine + got.astype(jnp.float32)


def on_device(
    points,
    counts,
    input_gain,
    key_weight,
    value_weight,
    query_weight,
    output_weight,
    middle_gain,
    up_weight,
    down_weight,
):
    block = points[0]
    rows = block.shape[0]
    width = block.shape[1]
    heads = width // HEAD_DIM
    sections = lax.axis_size("sec")
    blocks = lax.axis_size("pts")
    me = lax.axis_index("sec")

    stacked = jnp.concatenate([key_weight[0], value_weight[0]], axis=1)
    weights = gather_a2a(stacked, "pts", blocks).reshape(width, 2 * width)

    late_block, late_gain, weights = lax.optimization_barrier((block, input_gain[0], weights))
    query_block = from_last(late_block, "sec", sections)
    query_gain = from_last(late_gain, "sec", sections)

    normed = layer_normalizer(block.astype(jnp.float32), input_gain[0]).astype(jnp.bfloat16)
    projected = jnp.dot(normed, weights, preferred_element_type=jnp.float32)
    valid = jnp.arange(rows) < counts[0, 0]
    key_feats = feature_map(projected[:, :width]).astype(jnp.bfloat16)
    key_feats = jnp.where(valid[:, None], key_feats, jnp.zeros_like(key_feats))
    value_rows = projected[:, width:].astype(jnp.bfloat16)
    crossed = lax.dot_general(
        key_feats, value_rows, (((0,), (0,)), ((), ())), preferred_element_type=jnp.float32
    )
    local_state = jnp.concatenate(
        [
            crossed[h * HEAD_DIM : (h + 1) * HEAD_DIM, h * HEAD_DIM : (h + 1) * HEAD_DIM]
            for h in range(heads)
        ],
        axis=0,
    )
    local_total = jnp.sum(key_feats.astype(jnp.float32), axis=0).reshape(heads, HEAD_DIM)

    packed_rows = width + heads
    piece = -(-packed_rows // blocks)
    packed = jnp.concatenate(
        [
            local_state,
            local_total,
            jnp.zeros((piece * blocks - packed_rows, HEAD_DIM), jnp.float32),
        ],
        axis=0,
    ).reshape(blocks, piece, HEAD_DIM)
    reduced = jnp.sum(lax.all_to_all(packed, "pts", 0, 0, tiled=False), axis=0)
    by_section = gather_a2a(reduced.astype(jnp.bfloat16), "sec", sections)
    whole = gather_a2a(by_section, "pts", blocks).astype(jnp.float32)
    whole = whole.transpose(1, 0, 2, 3).reshape(sections, blocks * piece, HEAD_DIM)
    state_heads = whole[:, :width].reshape(sections, heads, HEAD_DIM, HEAD_DIM)
    total_heads = whole[:, width:packed_rows].reshape(sections, heads, HEAD_DIM)

    query_normed = layer_normalizer(query_block.astype(jnp.float32), query_gain).astype(
        jnp.bfloat16
    )
    query_feats = feature_map(
        jnp.dot(query_normed, query_weight, preferred_element_type=jnp.float32)
    ).astype(jnp.bfloat16)
    per_head_queries = query_feats.astype(jnp.float32).reshape(rows, heads, HEAD_DIM)
    numerator = jnp.einsum(
        "rhk,shkv->srhv", per_head_queries, state_heads, precision=lax.Precision.HIGH
    )
    denom = jnp.einsum(
        "rhk,shk->srh", per_head_queries, total_heads, precision=lax.Precision.HIGH
    )
    attended = (
        jnp.sum(numerator / denom[:, :, :, None], axis=0).reshape(rows, width).astype(jnp.bfloat16)
    )
    mixed = query_block.astype(jnp.float32) + jnp.dot(
        attended, output_weight, preferred_element_type=jnp.float32
    )
    centred = layer_normalizer(mixed, middle_gain).astype(jnp.bfloat16)
    hidden = jax.nn.gelu(
        jnp.dot(centred, up_weight, preferred_element_type=jnp.float32), approximate=True
    ).astype(jnp.bfloat16)
    term = jnp.dot(hidden, down_weight, preferred_element_type=jnp.float32)
    share = width // sections
    own_mixed = lax.dynamic_slice_in_dim(mixed, me * share, share, axis=1)
    return (own_mixed + scatter_sum(term, me, sections)).astype(jnp.bfloat16)


def solution(mesh):
    placed = (
        P("sec", "pts", None),
        P("sec", "pts"),
        P("sec", None),
        P("sec", "pts", None),
        P("sec", "pts", None),
        P(),
        P(),
        P(),
        P(None, "sec"),
        P("sec", None),
    )
    return jax.shard_map(
        on_device, mesh=mesh, in_specs=placed, out_specs=P("pts", "sec"), check_vma=False
    )
```

```python
import jax
import jax.numpy as jnp
from jax import lax
from jax.sharding import PartitionSpec as P

HEAD_DIM = 128


def layer_normalizer(values, gain):
    mean = jnp.mean(values, axis=-1, keepdims=True)
    centred = values - mean
    spread = jnp.mean(centred * centred, axis=-1, keepdims=True)
    return centred * lax.rsqrt(spread + 1e-05) * gain


def feature_map(values):
    return jax.nn.elu(values) + 1.0


def from_last(value, axis, sections):
    me = lax.axis_index(axis)
    last = sections - 1
    if sections != 4:
        out = value
        for target in range(last):
            got = lax.ppermute(value, axis, [(last, target)])
            out = jnp.where(me == target, got, out)
        return out
    far = lax.ppermute(value, axis, [(3, 1)])
    near = lax.ppermute(value, axis, [(3, 2)])
    farther = lax.ppermute(far, axis, [(1, 0)])
    return jnp.where(
        me == 3, value, jnp.where(me == 2, near, jnp.where(me == 1, far, farther))
    )


def gather_a2a(value, axis, count):
    spread = jnp.broadcast_to(value[None], (count,) + value.shape)
    return lax.all_to_all(spread, axis, 0, 0, tiled=False)


def gather_sec(value, me, sections):
    if sections != 4:
        return gather_a2a(value, "sec", sections)
    got = lax.ppermute(value, "sec", [(0, 1), (1, 0), (2, 3), (3, 2)])
    first = me % 2 == 0
    pair = jnp.where(first, jnp.stack([value, got]), jnp.stack([got, value]))
    other = lax.ppermute(pair, "sec", [(0, 2), (2, 0), (1, 3), (3, 1)])
    lower = me // 2 == 0
    return jnp.where(lower, jnp.concatenate([pair, other]), jnp.concatenate([other, pair]))


def scatter_sum(term, me, sections):
    rows, width = term.shape
    share = width // sections
    if sections != 4:
        parts = term.astype(jnp.bfloat16).reshape(rows, sections, share).transpose(1, 0, 2)
        got = lax.all_to_all(parts, "sec", 0, 0, tiled=False)
        return jnp.sum(got.astype(jnp.float32), axis=0)
    parity = me % 2
    quarters = term.reshape(rows, 2, 2, share)
    kept = lax.dynamic_index_in_dim(quarters, parity, axis=2, keepdims=False)
    sent = lax.dynamic_index_in_dim(quarters, 1 - parity, axis=2, keepdims=False)
    got = lax.ppermute(sent.astype(jnp.bfloat16), "sec", [(0, 1), (1, 0), (2, 3), (3, 2)])
    chip = kept + got.astype(jnp.float32)
    side = me // 2
    mine = lax.dynamic_index_in_dim(chip, side, axis=1, keepdims=False)
    other = lax.dynamic_index_in_dim(chip, 1 - side, axis=1, keepdims=False)
    got = lax.ppermute(other.astype(jnp.bfloat16), "sec", [(0, 2), (2, 0), (1, 3), (3, 1)])
    return mine + got.astype(jnp.float32)


def on_device(
    points,
    counts,
    input_gain,
    key_weight,
    value_weight,
    query_weight,
    output_weight,
    middle_gain,
    up_weight,
    down_weight,
):
    block = points[0]
    rows = block.shape[0]
    width = block.shape[1]
    heads = width // HEAD_DIM
    sections = lax.axis_size("sec")
    blocks = lax.axis_size("pts")
    me = lax.axis_index("sec")

    stacked = jnp.concatenate([key_weight[0], value_weight[0]], axis=1)
    weights = gather_a2a(stacked, "pts", blocks).reshape(width, 2 * width)

    query_block = from_last(block, "sec", sections)
    query_gain = from_last(input_gain[0], "sec", sections)

    normed = layer_normalizer(block.astype(jnp.float32), input_gain[0]).astype(jnp.bfloat16)
    projected = jnp.dot(normed, weights, preferred_element_type=jnp.float32)
    valid = jnp.arange(rows) < counts[0, 0]
    key_feats = feature_map(projected[:, :width]).astype(jnp.bfloat16)
    key_feats = jnp.where(valid[:, None], key_feats, jnp.zeros_like(key_feats))
    value_rows = projected[:, width:].astype(jnp.bfloat16)
    crossed = lax.dot_general(
        key_feats, value_rows, (((0,), (0,)), ((), ())), preferred_element_type=jnp.float32
    )
    local_state = jnp.concatenate(
        [
            crossed[h * HEAD_DIM : (h + 1) * HEAD_DIM, h * HEAD_DIM : (h + 1) * HEAD_DIM]
            for h in range(heads)
        ],
        axis=0,
    )
    local_total = jnp.sum(key_feats.astype(jnp.float32), axis=0).reshape(heads, HEAD_DIM)

    packed_rows = width + heads
    piece = -(-packed_rows // blocks)
    packed = jnp.concatenate(
        [
            local_state,
            local_total,
            jnp.zeros((piece * blocks - packed_rows, HEAD_DIM), jnp.float32),
        ],
        axis=0,
    ).reshape(blocks, piece, HEAD_DIM)
    reduced = jnp.sum(lax.all_to_all(packed, "pts", 0, 0, tiled=False), axis=0)
    by_section = gather_sec(reduced.astype(jnp.bfloat16), me, sections)
    whole = gather_a2a(by_section, "pts", blocks).astype(jnp.float32)
    whole = whole.transpose(1, 0, 2, 3).reshape(sections, blocks * piece, HEAD_DIM)
    state_heads = whole[:, :width].reshape(sections, heads, HEAD_DIM, HEAD_DIM)
    total_heads = whole[:, width:packed_rows].reshape(sections, heads, HEAD_DIM)

    query_normed = layer_normalizer(query_block.astype(jnp.float32), query_gain).astype(
        jnp.bfloat16
    )
    query_feats = feature_map(
        jnp.dot(query_normed, query_weight, preferred_element_type=jnp.float32)
    ).astype(jnp.bfloat16)
    per_head_queries = query_feats.astype(jnp.float32).reshape(rows, heads, HEAD_DIM)
    numerator = jnp.einsum(
        "rhk,shkv->srhv", per_head_queries, state_heads, precision=lax.Precision.HIGH
    )
    denom = jnp.einsum(
        "rhk,shk->srh", per_head_queries, total_heads, precision=lax.Precision.HIGH
    )
    attended = (
        jnp.sum(numerator / denom[:, :, :, None], axis=0).reshape(rows, width).astype(jnp.bfloat16)
    )
    mixed = query_block.astype(jnp.float32) + jnp.dot(
        attended, output_weight, preferred_element_type=jnp.float32
    )
    centred = layer_normalizer(mixed, middle_gain).astype(jnp.bfloat16)
    hidden = jax.nn.gelu(
        jnp.dot(centred, up_weight, preferred_element_type=jnp.float32), approximate=True
    ).astype(jnp.bfloat16)
    term = jnp.dot(hidden, down_weight, preferred_element_type=jnp.float32)
    share = width // sections
    own_mixed = lax.dynamic_slice_in_dim(mixed, me * share, share, axis=1)
    return (own_mixed + scatter_sum(term, me, sections)).astype(jnp.bfloat16)


def solution(mesh):
    placed = (
        P("sec", "pts", None),
        P("sec", "pts"),
        P("sec", None),
        P("sec", "pts", None),
        P("sec", "pts", None),
        P(),
        P(),
        P(),
        P(None, "sec"),
        P("sec", None),
    )
    return jax.shard_map(
        on_device, mesh=mesh, in_specs=placed, out_specs=P("pts", "sec"), check_vma=False
    )
```

```python
import jax
import jax.numpy as jnp
from jax import lax
from jax.sharding import PartitionSpec as P

HEAD_DIM = 128


def layer_normalizer(values, gain):
    mean = jnp.mean(values, axis=-1, keepdims=True)
    centred = values - mean
    spread = jnp.mean(centred * centred, axis=-1, keepdims=True)
    return centred * lax.rsqrt(spread + 1e-05) * gain


def feature_map(values):
    return jax.nn.elu(values) + 1.0


def from_last(value, axis, sections):
    me = lax.axis_index(axis)
    last = sections - 1
    if sections != 4:
        out = value
        for target in range(last):
            got = lax.ppermute(value, axis, [(last, target)])
            out = jnp.where(me == target, got, out)
        return out
    far = lax.ppermute(value, axis, [(3, 1)])
    near = lax.ppermute(value, axis, [(3, 2)])
    farther = lax.ppermute(far, axis, [(1, 0)])
    return jnp.where(
        me == 3, value, jnp.where(me == 2, near, jnp.where(me == 1, far, farther))
    )


def gather_a2a(value, axis, count):
    spread = jnp.broadcast_to(value[None], (count,) + value.shape)
    return lax.all_to_all(spread, axis, 0, 0, tiled=False)


def gather_sec(value, me, sections):
    if sections != 4:
        return gather_a2a(value, "sec", sections)
    got = lax.ppermute(value, "sec", [(0, 1), (1, 0), (2, 3), (3, 2)])
    first = me % 2 == 0
    pair = jnp.where(first, jnp.stack([value, got]), jnp.stack([got, value]))
    other = lax.ppermute(pair, "sec", [(0, 2), (2, 0), (1, 3), (3, 1)])
    lower = me // 2 == 0
    return jnp.where(lower, jnp.concatenate([pair, other]), jnp.concatenate([other, pair]))


def scatter_sum(term, me, sections):
    rows, width = term.shape
    share = width // sections
    if sections != 4:
        parts = term.astype(jnp.bfloat16).reshape(rows, sections, share).transpose(1, 0, 2)
        got = lax.all_to_all(parts, "sec", 0, 0, tiled=False)
        return jnp.sum(got.astype(jnp.float32), axis=0)
    parity = me % 2
    quarters = term.reshape(rows, 2, 2, share)
    kept = lax.dynamic_index_in_dim(quarters, parity, axis=2, keepdims=False)
    sent = lax.dynamic_index_in_dim(quarters, 1 - parity, axis=2, keepdims=False)
    got = lax.ppermute(sent.astype(jnp.bfloat16), "sec", [(0, 1), (1, 0), (2, 3), (3, 2)])
    chip = kept + got.astype(jnp.float32)
    side = me // 2
    mine = lax.dynamic_index_in_dim(chip, side, axis=1, keepdims=False)
    other = lax.dynamic_index_in_dim(chip, 1 - side, axis=1, keepdims=False)
    got = lax.ppermute(other.astype(jnp.bfloat16), "sec", [(0, 2), (2, 0), (1, 3), (3, 1)])
    return mine + got.astype(jnp.float32)


def on_device(
    points,
    counts,
    input_gain,
    key_weight,
    value_weight,
    query_weight,
    output_weight,
    middle_gain,
    up_weight,
    down_weight,
):
    block = points[0]
    rows = block.shape[0]
    width = block.shape[1]
    heads = width // HEAD_DIM
    sections = lax.axis_size("sec")
    blocks = lax.axis_size("pts")
    me = lax.axis_index("sec")

    stacked = jnp.concatenate([key_weight[0], value_weight[0]], axis=1)
    weights = gather_a2a(stacked, "pts", blocks).reshape(width, 2 * width)

    query_block = from_last(block, "sec", sections)
    query_gain = from_last(input_gain[0], "sec", sections)

    normed = layer_normalizer(block.astype(jnp.float32), input_gain[0]).astype(jnp.bfloat16)
    projected = jnp.dot(normed, weights, preferred_element_type=jnp.float32)
    valid = jnp.arange(rows) < counts[0, 0]
    key_feats = feature_map(projected[:, :width]).astype(jnp.bfloat16)
    key_feats = jnp.where(valid[:, None], key_feats, jnp.zeros_like(key_feats))
    value_rows = projected[:, width:].astype(jnp.bfloat16)
    crossed = lax.dot_general(
        key_feats, value_rows, (((0,), (0,)), ((), ())), preferred_element_type=jnp.float32
    )
    local_state = jnp.concatenate(
        [
            crossed[h * HEAD_DIM : (h + 1) * HEAD_DIM, h * HEAD_DIM : (h + 1) * HEAD_DIM]
            for h in range(heads)
        ],
        axis=0,
    )
    local_total = jnp.sum(key_feats.astype(jnp.float32), axis=0).reshape(heads, HEAD_DIM)

    packed_rows = width + heads
    piece = -(-packed_rows // blocks)
    packed = jnp.concatenate(
        [
            local_state,
            local_total,
            jnp.zeros((piece * blocks - packed_rows, HEAD_DIM), jnp.float32),
        ],
        axis=0,
    ).reshape(blocks, piece, HEAD_DIM)
    reduced = jnp.sum(lax.all_to_all(packed, "pts", 0, 0, tiled=False), axis=0)
    by_section = gather_sec(reduced.astype(jnp.bfloat16), me, sections)
    whole = gather_a2a(by_section, "pts", blocks).astype(jnp.float32)
    whole = whole.transpose(1, 0, 2, 3).reshape(sections, blocks * piece, HEAD_DIM)
    state_heads = whole[:, :width].reshape(sections, heads, HEAD_DIM, HEAD_DIM)
    total_heads = whole[:, width:packed_rows].reshape(sections, heads, HEAD_DIM)

    query_normed = layer_normalizer(query_block.astype(jnp.float32), query_gain).astype(
        jnp.bfloat16
    )
    query_feats = feature_map(
        jnp.dot(query_normed, query_weight, preferred_element_type=jnp.float32)
    ).astype(jnp.bfloat16)
    per_head_queries = query_feats.astype(jnp.float32).reshape(rows, heads, HEAD_DIM)
    numerator = jnp.einsum(
        "rhk,shkv->srhv", per_head_queries, state_heads, precision=lax.Precision.HIGH
    )
    denom = jnp.einsum(
        "rhk,shk->srh", per_head_queries, total_heads, precision=lax.Precision.HIGH
    )
    attended = (
        jnp.sum(numerator / denom[:, :, :, None], axis=0).reshape(rows, width).astype(jnp.bfloat16)
    )
    mixed = query_block.astype(jnp.float32) + jnp.dot(
        attended, output_weight, preferred_element_type=jnp.float32
    )
    centred = layer_normalizer(mixed, middle_gain).astype(jnp.bfloat16)
    hidden = jax.nn.gelu(
        jnp.dot(centred, up_weight, preferred_element_type=jnp.float32), approximate=True
    ).astype(jnp.bfloat16)
    share = width // sections
    own_mixed = lax.dynamic_slice_in_dim(mixed, me * share, share, axis=1)
    if sections != 4:
        term = jnp.dot(hidden, down_weight, preferred_element_type=jnp.float32)
        return (own_mixed + scatter_sum(term, me, sections)).astype(jnp.bfloat16)
    side = me // 2
    parity = me % 2
    quarters = down_weight.reshape(down_weight.shape[0], 2, 2, share)
    on_chip = [(0, 1), (1, 0), (2, 3), (3, 2)]

    def half_of(which):
        weights_half = lax.dynamic_index_in_dim(quarters, which, axis=1, keepdims=False)
        made = jnp.einsum("rf,fps->rps", hidden, weights_half, preferred_element_type=jnp.float32)
        kept = lax.dynamic_index_in_dim(made, parity, axis=1, keepdims=False)
        sent = lax.dynamic_index_in_dim(made, 1 - parity, axis=1, keepdims=False)
        return kept + lax.ppermute(sent.astype(jnp.bfloat16), "sec", on_chip).astype(jnp.float32)

    crossing = half_of(1 - side)
    arrived = lax.ppermute(crossing.astype(jnp.bfloat16), "sec", [(0, 2), (2, 0), (1, 3), (3, 1)])
    staying = half_of(side)
    return (own_mixed + staying + arrived.astype(jnp.float32)).astype(jnp.bfloat16)


def solution(mesh):
    placed = (
        P("sec", "pts", None),
        P("sec", "pts"),
        P("sec", None),
        P("sec", "pts", None),
        P("sec", "pts", None),
        P(),
        P(),
        P(),
        P(None, "sec"),
        P("sec", None),
    )
    return jax.shard_map(
        on_device, mesh=mesh, in_specs=placed, out_specs=P("pts", "sec"), check_vma=False
    )
```

```python
import jax
import jax.numpy as jnp
from jax import lax
from jax.sharding import PartitionSpec as P

HEAD_DIM = 128


def layer_normalizer(values, gain):
    mean = jnp.mean(values, axis=-1, keepdims=True)
    centred = values - mean
    spread = jnp.mean(centred * centred, axis=-1, keepdims=True)
    return centred * lax.rsqrt(spread + 1e-05) * gain


def feature_map(values):
    return jax.nn.elu(values) + 1.0


def from_last(value, axis, sections):
    me = lax.axis_index(axis)
    last = sections - 1
    if sections != 4:
        out = value
        for target in range(last):
            got = lax.ppermute(value, axis, [(last, target)])
            out = jnp.where(me == target, got, out)
        return out
    far = lax.ppermute(value, axis, [(3, 1)])
    near = lax.ppermute(value, axis, [(3, 2)])
    farther = lax.ppermute(far, axis, [(1, 0)])
    return jnp.where(
        me == 3, value, jnp.where(me == 2, near, jnp.where(me == 1, far, farther))
    )


def gather_a2a(value, axis, count):
    spread = jnp.broadcast_to(value[None], (count,) + value.shape)
    return lax.all_to_all(spread, axis, 0, 0, tiled=False)


def gather_sec(value, me, sections):
    if sections != 4:
        return gather_a2a(value, "sec", sections)
    got = lax.ppermute(value, "sec", [(0, 1), (1, 0), (2, 3), (3, 2)])
    first = me % 2 == 0
    pair = jnp.where(first, jnp.stack([value, got]), jnp.stack([got, value]))
    other = lax.ppermute(pair, "sec", [(0, 2), (2, 0), (1, 3), (3, 1)])
    lower = me // 2 == 0
    return jnp.where(lower, jnp.concatenate([pair, other]), jnp.concatenate([other, pair]))


def scatter_sum(term, me, sections):
    rows, width = term.shape
    share = width // sections
    if sections != 4:
        parts = term.astype(jnp.bfloat16).reshape(rows, sections, share).transpose(1, 0, 2)
        got = lax.all_to_all(parts, "sec", 0, 0, tiled=False)
        return jnp.sum(got.astype(jnp.float32), axis=0)
    parity = me % 2
    quarters = term.reshape(rows, 2, 2, share)
    kept = lax.dynamic_index_in_dim(quarters, parity, axis=2, keepdims=False)
    sent = lax.dynamic_index_in_dim(quarters, 1 - parity, axis=2, keepdims=False)
    got = lax.ppermute(sent.astype(jnp.bfloat16), "sec", [(0, 1), (1, 0), (2, 3), (3, 2)])
    chip = kept + got.astype(jnp.float32)
    side = me // 2
    mine = lax.dynamic_index_in_dim(chip, side, axis=1, keepdims=False)
    other = lax.dynamic_index_in_dim(chip, 1 - side, axis=1, keepdims=False)
    got = lax.ppermute(other.astype(jnp.bfloat16), "sec", [(0, 2), (2, 0), (1, 3), (3, 1)])
    return mine + got.astype(jnp.float32)


def on_device(
    points,
    counts,
    input_gain,
    key_weight,
    value_weight,
    query_weight,
    output_weight,
    middle_gain,
    up_weight,
    down_weight,
):
    block = points[0]
    rows = block.shape[0]
    width = block.shape[1]
    heads = width // HEAD_DIM
    sections = lax.axis_size("sec")
    blocks = lax.axis_size("pts")
    me = lax.axis_index("sec")

    stacked = jnp.concatenate([key_weight[0], value_weight[0]], axis=1)
    spread = jnp.broadcast_to(stacked[None], (blocks,) + stacked.shape)
    spread, first_block = lax.optimization_barrier((spread, block))
    weights = lax.all_to_all(spread, "pts", 0, 0, tiled=False).reshape(width, 2 * width)

    query_block = from_last(first_block, "sec", sections)
    query_gain = from_last(input_gain[0], "sec", sections)

    normed = layer_normalizer(block.astype(jnp.float32), input_gain[0]).astype(jnp.bfloat16)
    projected = jnp.dot(normed, weights, preferred_element_type=jnp.float32)
    valid = jnp.arange(rows) < counts[0, 0]
    key_feats = feature_map(projected[:, :width]).astype(jnp.bfloat16)
    key_feats = jnp.where(valid[:, None], key_feats, jnp.zeros_like(key_feats))
    value_rows = projected[:, width:].astype(jnp.bfloat16)
    crossed = lax.dot_general(
        key_feats, value_rows, (((0,), (0,)), ((), ())), preferred_element_type=jnp.float32
    )
    local_state = jnp.concatenate(
        [
            crossed[h * HEAD_DIM : (h + 1) * HEAD_DIM, h * HEAD_DIM : (h + 1) * HEAD_DIM]
            for h in range(heads)
        ],
        axis=0,
    )
    local_total = jnp.sum(key_feats.astype(jnp.float32), axis=0).reshape(heads, HEAD_DIM)

    packed_rows = width + heads
    piece = -(-packed_rows // blocks)
    packed = jnp.concatenate(
        [
            local_state,
            local_total,
            jnp.zeros((piece * blocks - packed_rows, HEAD_DIM), jnp.float32),
        ],
        axis=0,
    ).reshape(blocks, piece, HEAD_DIM)
    reduced = jnp.sum(lax.all_to_all(packed, "pts", 0, 0, tiled=False), axis=0)
    by_section = gather_sec(reduced.astype(jnp.bfloat16), me, sections)
    whole = gather_a2a(by_section, "pts", blocks).astype(jnp.float32)
    whole = whole.transpose(1, 0, 2, 3).reshape(sections, blocks * piece, HEAD_DIM)
    state_heads = whole[:, :width].reshape(sections, heads, HEAD_DIM, HEAD_DIM)
    total_heads = whole[:, width:packed_rows].reshape(sections, heads, HEAD_DIM)

    query_normed = layer_normalizer(query_block.astype(jnp.float32), query_gain).astype(
        jnp.bfloat16
    )
    query_feats = feature_map(
        jnp.dot(query_normed, query_weight, preferred_element_type=jnp.float32)
    ).astype(jnp.bfloat16)
    per_head_queries = query_feats.astype(jnp.float32).reshape(rows, heads, HEAD_DIM)
    numerator = jnp.einsum(
        "rhk,shkv->srhv", per_head_queries, state_heads, precision=lax.Precision.HIGH
    )
    denom = jnp.einsum(
        "rhk,shk->srh", per_head_queries, total_heads, precision=lax.Precision.HIGH
    )
    attended = (
        jnp.sum(numerator / denom[:, :, :, None], axis=0).reshape(rows, width).astype(jnp.bfloat16)
    )
    mixed = query_block.astype(jnp.float32) + jnp.dot(
        attended, output_weight, preferred_element_type=jnp.float32
    )
    centred = layer_normalizer(mixed, middle_gain).astype(jnp.bfloat16)
    hidden = jax.nn.gelu(
        jnp.dot(centred, up_weight, preferred_element_type=jnp.float32), approximate=True
    ).astype(jnp.bfloat16)
    term = jnp.dot(hidden, down_weight, preferred_element_type=jnp.float32)
    share = width // sections
    own_mixed = lax.dynamic_slice_in_dim(mixed, me * share, share, axis=1)
    return (own_mixed + scatter_sum(term, me, sections)).astype(jnp.bfloat16)


def solution(mesh):
    placed = (
        P("sec", "pts", None),
        P("sec", "pts"),
        P("sec", None),
        P("sec", "pts", None),
        P("sec", "pts", None),
        P(),
        P(),
        P(),
        P(None, "sec"),
        P("sec", None),
    )
    return jax.shard_map(
        on_device, mesh=mesh, in_specs=placed, out_specs=P("pts", "sec"), check_vma=False
    )
```

```python
import jax
import jax.numpy as jnp
from jax import lax
from jax.sharding import PartitionSpec as P

HEAD_DIM = 128


def layer_normalizer(values, gain):
    mean = jnp.mean(values, axis=-1, keepdims=True)
    centred = values - mean
    spread = jnp.mean(centred * centred, axis=-1, keepdims=True)
    return centred * lax.rsqrt(spread + 1e-05) * gain


def feature_map(values):
    return jax.nn.elu(values) + 1.0


def from_last(value, axis, sections):
    me = lax.axis_index(axis)
    last = sections - 1
    if sections != 4:
        out = value
        for target in range(last):
            got = lax.ppermute(value, axis, [(last, target)])
            out = jnp.where(me == target, got, out)
        return out
    far = lax.ppermute(value, axis, [(3, 1)])
    near = lax.ppermute(value, axis, [(3, 2)])
    farther = lax.ppermute(far, axis, [(1, 0)])
    return jnp.where(
        me == 3, value, jnp.where(me == 2, near, jnp.where(me == 1, far, farther))
    )


def gather_a2a(value, axis, count):
    spread = jnp.broadcast_to(value[None], (count,) + value.shape)
    return lax.all_to_all(spread, axis, 0, 0, tiled=False)


def gather_sec(value, me, sections):
    if sections != 4:
        return gather_a2a(value, "sec", sections)
    got = lax.ppermute(value, "sec", [(0, 1), (1, 0), (2, 3), (3, 2)])
    first = me % 2 == 0
    pair = jnp.where(first, jnp.stack([value, got]), jnp.stack([got, value]))
    other = lax.ppermute(pair, "sec", [(0, 2), (2, 0), (1, 3), (3, 1)])
    lower = me // 2 == 0
    return jnp.where(lower, jnp.concatenate([pair, other]), jnp.concatenate([other, pair]))


def scatter_sum(term, me, sections):
    rows, width = term.shape
    share = width // sections
    if sections != 4:
        parts = term.astype(jnp.bfloat16).reshape(rows, sections, share).transpose(1, 0, 2)
        got = lax.all_to_all(parts, "sec", 0, 0, tiled=False)
        return jnp.sum(got.astype(jnp.float32), axis=0)
    parity = me % 2
    quarters = term.reshape(rows, 2, 2, share)
    kept = lax.dynamic_index_in_dim(quarters, parity, axis=2, keepdims=False)
    sent = lax.dynamic_index_in_dim(quarters, 1 - parity, axis=2, keepdims=False)
    got = lax.ppermute(sent.astype(jnp.bfloat16), "sec", [(0, 1), (1, 0), (2, 3), (3, 2)])
    chip = kept + got.astype(jnp.float32)
    side = me // 2
    mine = lax.dynamic_index_in_dim(chip, side, axis=1, keepdims=False)
    other = lax.dynamic_index_in_dim(chip, 1 - side, axis=1, keepdims=False)
    got = lax.ppermute(other.astype(jnp.bfloat16), "sec", [(0, 2), (2, 0), (1, 3), (3, 1)])
    return mine + got.astype(jnp.float32)


def on_device(
    points,
    counts,
    input_gain,
    key_weight,
    value_weight,
    query_weight,
    output_weight,
    middle_gain,
    up_weight,
    down_weight,
):
    block = points[0]
    rows = block.shape[0]
    width = block.shape[1]
    heads = width // HEAD_DIM
    sections = lax.axis_size("sec")
    blocks = lax.axis_size("pts")
    me = lax.axis_index("sec")

    stacked = jnp.concatenate([key_weight[0], value_weight[0]], axis=1)
    weights = gather_a2a(stacked, "pts", blocks).reshape(width, 2 * width)

    query_block = from_last(block, "sec", sections)
    query_gain = from_last(input_gain[0], "sec", sections)

    normed = layer_normalizer(block.astype(jnp.float32), input_gain[0]).astype(jnp.bfloat16)
    valid = jnp.arange(rows) < counts[0, 0]
    key_feats = feature_map(
        jnp.dot(normed, weights[:, :width], preferred_element_type=jnp.float32)
    ).astype(jnp.bfloat16)
    key_feats = jnp.where(valid[:, None], key_feats, jnp.zeros_like(key_feats))
    value_rows = jnp.dot(normed, weights[:, width:], preferred_element_type=jnp.float32).astype(
        jnp.bfloat16
    )
    crossed = lax.dot_general(
        key_feats, value_rows, (((0,), (0,)), ((), ())), preferred_element_type=jnp.float32
    )
    local_state = jnp.concatenate(
        [
            crossed[h * HEAD_DIM : (h + 1) * HEAD_DIM, h * HEAD_DIM : (h + 1) * HEAD_DIM]
            for h in range(heads)
        ],
        axis=0,
    )
    local_total = jnp.sum(key_feats.astype(jnp.float32), axis=0).reshape(heads, HEAD_DIM)

    packed_rows = width + heads
    piece = -(-packed_rows // blocks)
    packed = jnp.concatenate(
        [
            local_state,
            local_total,
            jnp.zeros((piece * blocks - packed_rows, HEAD_DIM), jnp.float32),
        ],
        axis=0,
    ).reshape(blocks, piece, HEAD_DIM)
    reduced = jnp.sum(lax.all_to_all(packed, "pts", 0, 0, tiled=False), axis=0)
    by_section = gather_sec(reduced.astype(jnp.bfloat16), me, sections)
    whole = gather_a2a(by_section, "pts", blocks).astype(jnp.float32)
    whole = whole.transpose(1, 0, 2, 3).reshape(sections, blocks * piece, HEAD_DIM)
    state_heads = whole[:, :width].reshape(sections, heads, HEAD_DIM, HEAD_DIM)
    total_heads = whole[:, width:packed_rows].reshape(sections, heads, HEAD_DIM)

    query_normed = layer_normalizer(query_block.astype(jnp.float32), query_gain).astype(
        jnp.bfloat16
    )
    query_feats = feature_map(
        jnp.dot(query_normed, query_weight, preferred_element_type=jnp.float32)
    ).astype(jnp.bfloat16)
    per_head_queries = query_feats.astype(jnp.float32).reshape(rows, heads, HEAD_DIM)
    numerator = jnp.einsum(
        "rhk,shkv->srhv", per_head_queries, state_heads, precision=lax.Precision.HIGH
    )
    denom = jnp.einsum(
        "rhk,shk->srh", per_head_queries, total_heads, precision=lax.Precision.HIGH
    )
    attended = (
        jnp.sum(numerator / denom[:, :, :, None], axis=0).reshape(rows, width).astype(jnp.bfloat16)
    )
    mixed = query_block.astype(jnp.float32) + jnp.dot(
        attended, output_weight, preferred_element_type=jnp.float32
    )
    centred = layer_normalizer(mixed, middle_gain).astype(jnp.bfloat16)
    hidden = jax.nn.gelu(
        jnp.dot(centred, up_weight, preferred_element_type=jnp.float32), approximate=True
    ).astype(jnp.bfloat16)
    term = jnp.dot(hidden, down_weight, preferred_element_type=jnp.float32)
    share = width // sections
    own_mixed = lax.dynamic_slice_in_dim(mixed, me * share, share, axis=1)
    return (own_mixed + scatter_sum(term, me, sections)).astype(jnp.bfloat16)


def solution(mesh):
    placed = (
        P("sec", "pts", None),
        P("sec", "pts"),
        P("sec", None),
        P("sec", "pts", None),
        P("sec", "pts", None),
        P(),
        P(),
        P(),
        P(None, "sec"),
        P("sec", None),
    )
    return jax.shard_map(
        on_device, mesh=mesh, in_specs=placed, out_specs=P("pts", "sec"), check_vma=False
    )
```

```python
import jax
import jax.numpy as jnp
from jax import lax
from jax.sharding import PartitionSpec as P

HEAD_DIM = 128


def layer_normalizer(values, gain):
    mean = jnp.mean(values, axis=-1, keepdims=True)
    centred = values - mean
    spread = jnp.mean(centred * centred, axis=-1, keepdims=True)
    return centred * lax.rsqrt(spread + 1e-05) * gain


def feature_map(values):
    return jax.nn.elu(values) + 1.0


def from_last(value, axis, sections):
    me = lax.axis_index(axis)
    last = sections - 1
    if sections != 4:
        out = value
        for target in range(last):
            got = lax.ppermute(value, axis, [(last, target)])
            out = jnp.where(me == target, got, out)
        return out
    far = lax.ppermute(value, axis, [(3, 1)])
    near = lax.ppermute(value, axis, [(3, 2)])
    farther = lax.ppermute(far, axis, [(1, 0)])
    return jnp.where(
        me == 3, value, jnp.where(me == 2, near, jnp.where(me == 1, far, farther))
    )


def gather_a2a(value, axis, count):
    spread = jnp.broadcast_to(value[None], (count,) + value.shape)
    return lax.all_to_all(spread, axis, 0, 0, tiled=False)


def gather_sec(value, me, sections):
    if sections != 4:
        return gather_a2a(value, "sec", sections)
    got = lax.ppermute(value, "sec", [(0, 1), (1, 0), (2, 3), (3, 2)])
    first = me % 2 == 0
    pair = jnp.where(first, jnp.stack([value, got]), jnp.stack([got, value]))
    other = lax.ppermute(pair, "sec", [(0, 2), (2, 0), (1, 3), (3, 1)])
    lower = me // 2 == 0
    return jnp.where(lower, jnp.concatenate([pair, other]), jnp.concatenate([other, pair]))


def scatter_sum(term, me, sections):
    rows, width = term.shape
    share = width // sections
    if sections != 4:
        parts = term.astype(jnp.bfloat16).reshape(rows, sections, share).transpose(1, 0, 2)
        got = lax.all_to_all(parts, "sec", 0, 0, tiled=False)
        return jnp.sum(got.astype(jnp.float32), axis=0)
    parity = me % 2
    quarters = term.reshape(rows, 2, 2, share)
    kept = lax.dynamic_index_in_dim(quarters, parity, axis=2, keepdims=False)
    sent = lax.dynamic_index_in_dim(quarters, 1 - parity, axis=2, keepdims=False)
    got = lax.ppermute(sent.astype(jnp.bfloat16), "sec", [(0, 1), (1, 0), (2, 3), (3, 2)])
    chip = kept + got.astype(jnp.float32)
    side = me // 2
    mine = lax.dynamic_index_in_dim(chip, side, axis=1, keepdims=False)
    other = lax.dynamic_index_in_dim(chip, 1 - side, axis=1, keepdims=False)
    got = lax.ppermute(other.astype(jnp.bfloat16), "sec", [(0, 2), (2, 0), (1, 3), (3, 1)])
    return mine + got.astype(jnp.float32)


def on_device(
    points,
    counts,
    input_gain,
    key_weight,
    value_weight,
    query_weight,
    output_weight,
    middle_gain,
    up_weight,
    down_weight,
):
    block = points[0]
    rows = block.shape[0]
    width = block.shape[1]
    heads = width // HEAD_DIM
    sections = lax.axis_size("sec")
    blocks = lax.axis_size("pts")
    me = lax.axis_index("sec")

    stacked = jnp.concatenate([key_weight[0], value_weight[0]], axis=1)
    weights = gather_a2a(stacked, "pts", blocks).reshape(width, 2 * width)

    query_block = from_last(points, "sec", sections)[0]
    query_gain = from_last(input_gain[0], "sec", sections)

    normed = layer_normalizer(block.astype(jnp.float32), input_gain[0]).astype(jnp.bfloat16)
    projected = jnp.dot(normed, weights, preferred_element_type=jnp.float32)
    valid = jnp.arange(rows) < counts[0, 0]
    key_feats = feature_map(projected[:, :width]).astype(jnp.bfloat16)
    key_feats = jnp.where(valid[:, None], key_feats, jnp.zeros_like(key_feats))
    value_rows = projected[:, width:].astype(jnp.bfloat16)
    crossed = lax.dot_general(
        key_feats, value_rows, (((0,), (0,)), ((), ())), preferred_element_type=jnp.float32
    )
    local_state = jnp.concatenate(
        [
            crossed[h * HEAD_DIM : (h + 1) * HEAD_DIM, h * HEAD_DIM : (h + 1) * HEAD_DIM]
            for h in range(heads)
        ],
        axis=0,
    )
    local_total = jnp.sum(key_feats.astype(jnp.float32), axis=0).reshape(heads, HEAD_DIM)

    packed_rows = width + heads
    piece = -(-packed_rows // blocks)
    packed = jnp.concatenate(
        [
            local_state,
            local_total,
            jnp.zeros((piece * blocks - packed_rows, HEAD_DIM), jnp.float32),
        ],
        axis=0,
    ).reshape(blocks, piece, HEAD_DIM)
    reduced = jnp.sum(lax.all_to_all(packed, "pts", 0, 0, tiled=False), axis=0)
    by_section = gather_sec(reduced.astype(jnp.bfloat16), me, sections)
    whole = gather_a2a(by_section, "pts", blocks).astype(jnp.float32)
    whole = whole.transpose(1, 0, 2, 3).reshape(sections, blocks * piece, HEAD_DIM)
    state_heads = whole[:, :width].reshape(sections, heads, HEAD_DIM, HEAD_DIM)
    total_heads = whole[:, width:packed_rows].reshape(sections, heads, HEAD_DIM)

    query_normed = layer_normalizer(query_block.astype(jnp.float32), query_gain).astype(
        jnp.bfloat16
    )
    query_feats = feature_map(
        jnp.dot(query_normed, query_weight, preferred_element_type=jnp.float32)
    ).astype(jnp.bfloat16)
    per_head_queries = query_feats.astype(jnp.float32).reshape(rows, heads, HEAD_DIM)
    numerator = jnp.einsum(
        "rhk,shkv->srhv", per_head_queries, state_heads, precision=lax.Precision.HIGH
    )
    denom = jnp.einsum(
        "rhk,shk->srh", per_head_queries, total_heads, precision=lax.Precision.HIGH
    )
    attended = (
        jnp.sum(numerator / denom[:, :, :, None], axis=0).reshape(rows, width).astype(jnp.bfloat16)
    )
    mixed = query_block.astype(jnp.float32) + jnp.dot(
        attended, output_weight, preferred_element_type=jnp.float32
    )
    centred = layer_normalizer(mixed, middle_gain).astype(jnp.bfloat16)
    hidden = jax.nn.gelu(
        jnp.dot(centred, up_weight, preferred_element_type=jnp.float32), approximate=True
    ).astype(jnp.bfloat16)
    term = jnp.dot(hidden, down_weight, preferred_element_type=jnp.float32)
    share = width // sections
    own_mixed = lax.dynamic_slice_in_dim(mixed, me * share, share, axis=1)
    return (own_mixed + scatter_sum(term, me, sections)).astype(jnp.bfloat16)


def solution(mesh):
    placed = (
        P("sec", "pts", None),
        P("sec", "pts"),
        P("sec", None),
        P("sec", "pts", None),
        P("sec", "pts", None),
        P(),
        P(),
        P(),
        P(None, "sec"),
        P("sec", None),
    )
    return jax.shard_map(
        on_device, mesh=mesh, in_specs=placed, out_specs=P("pts", "sec"), check_vma=False
    )
```
